512 devices in a mesh: col: 32 (over y, x, core), row: 16 (over z).
Axes of the slice: x: 4, y: 4, z: 16, core: 2. Of those that a mesh axis runs over, the one named last changes fastest.
Arguments:
- normal_matrix: float32 [4, 16, 128, 2, 32, 128], P(None, 'row', None, None, 'col'), may hold values from -3 to 5.5, as said below
- right_sides: float32 [256, 4, 16, 128], P('col', None, 'row'), may hold values from -6 to 6
Outputs:
- reduced_matrix: float32 [4, 16, 128, 2, 32, 128], P(None, 'row', None, None, 'col')
- reduced_sides: float32 [256, 4, 16, 128], P('col', None, 'row')
The draws below stay inside these ranges and needn't reach their ends.
Inputs may be any that keep to these rules, and one draw needn't show every extreme that they name: `normal_matrix`: A is symmetric; its leading 128 x 128 block is strictly diagonally dominant with a positive diagonal.
All inputs are finite; a program needn't handle non-finite values.
Results may differ from the reference program's by a relative error of at most 0.00005.
Values sent between devices are 32-bit elements; how exact they have to be, the bound alone decides.
No kernel may reach another device: no remote copies, remote signals or barrier semaphores. Data moves between devices by JAX's collectives and lax.ppermute only.
A program may use at most 64 MiB of HBM per device.

```python
import jax
import jax.numpy as jnp
from jax import lax

NB = 128
CB = 2
ROW_DEVS = 16
COL_DEVS = 32
RB = 4
M = 8192
R = 256


def draw_normal_matrix(key, part):
    first_key, second_key, third_key = jax.random.split(key, 3)
    size_total = CB * COL_DEVS * NB
    base = jnp.clip(jax.random.normal(first_key, (size_total, size_total), jnp.float32), -4.0, 4.0)
    offset = 0.3
    full = 0.5 * (base + base.T) * 0.70710678
    offdiag = jax.random.uniform(second_key, (NB, NB), jnp.float32, -1.0, 1.0)
    offdiag = (0.5 * (offdiag + offdiag.T) + offset) * (2.0 / NB)
    diagonal = 3.5 + 2.0 * jax.random.uniform(third_key, (NB,), jnp.float32)
    eye = jnp.eye(NB, dtype=jnp.float32)
    corner = offdiag * (1.0 - eye) + eye * diagonal[:, None]
    full = full.at[:NB, :NB].set(corner)
    return full.reshape(RB, ROW_DEVS, NB, CB, COL_DEVS, NB)


def steps_of(key, dims, cuts, low, high):
    gain = 1.0
    for dim, blocks in cuts:
        steps = jax.random.uniform(jax.random.fold_in(jax.random.fold_in(key, 6), dim), (blocks,), jnp.float32, low / len(cuts), high / len(cuts))
        gain = gain * jnp.repeat(jnp.exp(steps), dims[dim] // blocks).reshape((-1,) + (1,) * (len(dims) - 1 - dim))
    return gain


def noise(rng, dims, scale, reach, cuts=(), held_as=jnp.bfloat16):
    gain = steps_of(rng, dims, cuts, -0.22, 0.18) if cuts else 1.0
    values = jax.random.normal(rng, dims, jnp.float32) * scale * gain
    return jnp.minimum(jnp.maximum(values, -reach), reach).astype(held_as)


def setup_inputs(seed: int = 0) -> dict:
    key_list = jax.random.split(jax.random.key(seed), 3)
    normal_matrix = draw_normal_matrix(jax.random.fold_in(key_list[2], 71), 0)
    right_sides = noise(key_list[1], (R, RB, ROW_DEVS, NB), 1.0, 6.0, ((0, 32), (2, 16)), jnp.float32)
    return dict(normal_matrix=normal_matrix, right_sides=right_sides)


def reference(normal_matrix, right_sides):
    full = normal_matrix.reshape(M, M)
    corner = jnp.linalg.cholesky(full[:NB, :NB])
    panel = jax.scipy.linalg.solve_triangular(corner, full[:, :NB].T, lower=True).T
    change = jnp.dot(panel.astype(jnp.float32), panel.T.astype(jnp.float32), precision=lax.Precision.HIGHEST, preferred_element_type=jnp.float32)
    trailing = full - change
    ids = jnp.arange(M)
    inner = (ids[:, None] >= NB) & (ids[None, :] >= NB)
    result = jnp.where(inner, trailing, jnp.float32(0.0))
    column = panel.at[:NB].set(corner)
    result = result.at[:, :NB].set(column)
    sides = right_sides.reshape(R, M)
    lead = jax.scipy.linalg.solve_triangular(corner, sides[:, :NB].T, lower=True).T
    reduced = sides - jnp.dot(lead.astype(jnp.float32), panel.T.astype(jnp.float32), precision=lax.Precision.HIGHEST, preferred_element_type=jnp.float32)
    reduced = reduced.at[:, :NB].set(lead)
    return (result.reshape(normal_matrix.shape), reduced.reshape(right_sides.shape))
```

```python
import jax
import jax.numpy as jnp
from jax import lax
from jax.sharding import PartitionSpec as P


def spread(block, axis):
    count = lax.axis_size(axis)
    index = lax.axis_index(axis)
    step = 1
    while step < count:
        pairs = [(i, i + step) for i in range(step) if i + step < count]
        arrived = lax.ppermute(block, axis, pairs)
        block = jnp.where((index >= step) & (index < 2 * step), arrived, block)
        step *= 2
    return block


def on_device(normal_matrix, right_sides):
    row_blocks, _, block, col_blocks, _, _ = normal_matrix.shape
    col_id = lax.axis_index("col")
    row_id = lax.axis_index("row")
    col_count = lax.axis_size("col")
    row_count = lax.axis_size("row")
    side_count = right_sides.shape[0]
    local = normal_matrix.reshape(row_blocks * block, col_blocks * block)

    corner_raw = spread(spread(local[:block, :block], "row"), "col")
    left = spread(local[:, :block], "col")
    top = jnp.concatenate([local[:block], right_sides[:, 0, 0, :].T], axis=1)
    top = spread(top, "row")

    corner = jnp.linalg.cholesky(corner_raw)
    rhs = jnp.concatenate([left.T, top], axis=1)
    solved = jax.scipy.linalg.solve_triangular(corner, rhs, lower=True).T
    rows_factor = solved[: row_blocks * block]
    cols_factor = solved[row_blocks * block: (row_blocks + col_blocks) * block]
    lead = solved[(row_blocks + col_blocks) * block:]

    change = jnp.dot(
        rows_factor,
        cols_factor.T,
        precision=lax.Precision.HIGHEST,
        preferred_element_type=jnp.float32,
    )
    trailing = (local - change).reshape(row_blocks, block, col_blocks, block)
    global_rows = row_id + row_count * jnp.arange(row_blocks, dtype=jnp.int32)
    global_cols = col_id + col_count * jnp.arange(col_blocks, dtype=jnp.int32)
    inner = (global_rows[:, None, None, None] >= 1) & (global_cols[None, None, :, None] >= 1)
    result = jnp.where(inner, trailing, jnp.float32(0.0))
    column = jnp.where(
        global_rows[:, None, None] == 0, corner[None], rows_factor.reshape(row_blocks, block, block)
    )
    result = jnp.where((global_cols == 0)[None, None, :, None], column[:, :, None, :], result)
    result = result.reshape(normal_matrix.shape)

    flat = right_sides.reshape(side_count, row_blocks * block)
    reduced = flat - jnp.dot(
        lead, rows_factor.T, precision=lax.Precision.HIGHEST, preferred_element_type=jnp.float32
    )
    reduced = reduced.reshape(side_count, row_blocks, block)
    reduced = jnp.where((global_rows == 0)[None, :, None], lead[:, None, :], reduced)
    return (result, reduced.reshape(right_sides.shape))


def solution(mesh):
    placed = (P(None, "row", None, None, "col", None), P("col", None, "row", None))
    return jax.shard_map(
        on_device,
        mesh=mesh,
        in_specs=placed,
        out_specs=(P(None, "row", None, None, "col", None), P("col", None, "row", None)),
        check_vma=False,
    )
```

```python
import jax
import jax.numpy as jnp
from jax import lax
from jax.sharding import PartitionSpec as P


def spread(block, axis):
    count = lax.axis_size(axis)
    index = lax.axis_index(axis)
    step = 1
    while step < count:
        pairs = [(i, i + step) for i in range(step) if i + step < count]
        arrived = lax.ppermute(block, axis, pairs)
        block = jnp.where((index >= step) & (index < 2 * step), arrived, block)
        step *= 2
    return block


def on_device(normal_matrix, right_sides):
    row_blocks, _, block, col_blocks, _, _ = normal_matrix.shape
    col_id = lax.axis_index("col")
    row_id = lax.axis_index("row")
    col_count = lax.axis_size("col")
    row_count = lax.axis_size("row")
    side_count = right_sides.shape[0]
    local = normal_matrix.reshape(row_blocks * block, col_blocks * block)

    left = spread(local[:, :block], "col")
    top = jnp.concatenate([local[:block], right_sides[:, 0, 0, :].T], axis=1)
    top = spread(top, "row")
    corner_raw = spread(top[:, :block], "col")

    corner = jnp.linalg.cholesky(corner_raw)
    rhs = jnp.concatenate([left.T, top], axis=1)
    solved = jax.scipy.linalg.solve_triangular(corner, rhs, lower=True).T
    rows_factor = solved[: row_blocks * block]
    cols_factor = solved[row_blocks * block: (row_blocks + col_blocks) * block]
    lead = solved[(row_blocks + col_blocks) * block:]

    change = jnp.dot(
        rows_factor,
        cols_factor.T,
        precision=lax.Precision.HIGHEST,
        preferred_element_type=jnp.float32,
    )
    trailing = (local - change).reshape(row_blocks, block, col_blocks, block)
    global_rows = row_id + row_count * jnp.arange(row_blocks, dtype=jnp.int32)
    global_cols = col_id + col_count * jnp.arange(col_blocks, dtype=jnp.int32)
    inner = (global_rows[:, None, None, None] >= 1) & (global_cols[None, None, :, None] >= 1)
    result = jnp.where(inner, trailing, jnp.float32(0.0))
    column = jnp.where(
        global_rows[:, None, None] == 0, corner[None], rows_factor.reshape(row_blocks, block, block)
    )
    result = jnp.where((global_cols == 0)[None, None, :, None], column[:, :, None, :], result)
    result = result.reshape(normal_matrix.shape)

    flat = right_sides.reshape(side_count, row_blocks * block)
    reduced = flat - jnp.dot(
        lead, rows_factor.T, precision=lax.Precision.HIGHEST, preferred_element_type=jnp.float32
    )
    reduced = reduced.reshape(side_count, row_blocks, block)
    reduced = jnp.where((global_rows == 0)[None, :, None], lead[:, None, :], reduced)
    return (result, reduced.reshape(right_sides.shape))


def solution(mesh):
    placed = (P(None, "row", None, None, "col", None), P("col", None, "row", None))
    return jax.shard_map(
        on_device,
        mesh=mesh,
        in_specs=placed,
        out_specs=(P(None, "row", None, None, "col", None), P("col", None, "row", None)),
        check_vma=False,
    )
```

```python
import jax
import jax.numpy as jnp
from jax import lax
from jax.sharding import PartitionSpec as P


def spread(block, axis):
    count = lax.axis_size(axis)
    index = lax.axis_index(axis)
    step = 1
    while 2 * step < count:
        step *= 2
    while step >= 1:
        pairs = [(i, i + step) for i in range(0, count, 2 * step) if i + step < count]
        arrived = lax.ppermute(block, axis, pairs)
        block = jnp.where(index % (2 * step) == step, arrived, block)
        step //= 2
    return block


def on_device(normal_matrix, right_sides):
    row_blocks, _, block, col_blocks, _, _ = normal_matrix.shape
    col_id = lax.axis_index("col")
    row_id = lax.axis_index("row")
    col_count = lax.axis_size("col")
    row_count = lax.axis_size("row")
    side_count = right_sides.shape[0]
    local = normal_matrix.reshape(row_blocks * block, col_blocks * block)

    left = spread(local[:, :block], "col")
    top = jnp.concatenate([local[:block], right_sides[:, 0, 0, :].T], axis=1)
    top = spread(top, "row")
    corner_raw = spread(top[:, :block], "col")

    corner = jnp.linalg.cholesky(corner_raw)
    rhs = jnp.concatenate([left.T, top], axis=1)
    solved = jax.scipy.linalg.solve_triangular(corner, rhs, lower=True).T
    rows_factor = solved[: row_blocks * block]
    cols_factor = solved[row_blocks * block: (row_blocks + col_blocks) * block]
    lead = solved[(row_blocks + col_blocks) * block:]

    change = jnp.dot(
        rows_factor,
        cols_factor.T,
        precision=lax.Precision.HIGHEST,
        preferred_element_type=jnp.float32,
    )
    trailing = (local - change).reshape(row_blocks, block, col_blocks, block)
    global_rows = row_id + row_count * jnp.arange(row_blocks, dtype=jnp.int32)
    global_cols = col_id + col_count * jnp.arange(col_blocks, dtype=jnp.int32)
    inner = (global_rows[:, None, None, None] >= 1) & (global_cols[None, None, :, None] >= 1)
    result = jnp.where(inner, trailing, jnp.float32(0.0))
    column = jnp.where(
        global_rows[:, None, None] == 0, corner[None], rows_factor.reshape(row_blocks, block, block)
    )
    result = jnp.where((global_cols == 0)[None, None, :, None], column[:, :, None, :], result)
    result = result.reshape(normal_matrix.shape)

    flat = right_sides.reshape(side_count, row_blocks * block)
    reduced = flat - jnp.dot(
        lead, rows_factor.T, precision=lax.Precision.HIGHEST, preferred_element_type=jnp.float32
    )
    reduced = reduced.reshape(side_count, row_blocks, block)
    reduced = jnp.where((global_rows == 0)[None, :, None], lead[:, None, :], reduced)
    return (result, reduced.reshape(right_sides.shape))


def solution(mesh):
    placed = (P(None, "row", None, None, "col", None), P("col", None, "row", None))
    return jax.shard_map(
        on_device,
        mesh=mesh,
        in_specs=placed,
        out_specs=(P(None, "row", None, None, "col", None), P("col", None, "row", None)),
        check_vma=False,
    )
```

```python
import jax
import jax.numpy as jnp
from jax import lax
from jax.sharding import PartitionSpec as P


def spread(block, axis):
    count = lax.axis_size(axis)
    index = lax.axis_index(axis)
    step = 1
    while 2 * step < count:
        step *= 2
    while step >= 1:
        pairs = [(i, i + step) for i in range(0, count, 2 * step) if i + step < count]
        arrived = lax.ppermute(block, axis, pairs)
        block = jnp.where(index % (2 * step) == step, arrived, block)
        step //= 2
    return block


def spread_wide(block, axis):
    count = lax.axis_size(axis)
    index = lax.axis_index(axis)
    radices = []
    rest = count
    while rest > 1:
        radix = 4 if rest % 4 == 0 else rest
        radices.append(radix)
        rest //= radix
    span = count
    for radix in radices:
        span //= radix
        got = block
        for digit in range(1, radix):
            pairs = [(i, i + digit * span) for i in range(0, count, span * radix)]
            arrived = lax.ppermute(block, axis, pairs)
            mine = (index % (span * radix)) == digit * span
            got = jnp.where(mine, arrived, got)
        block = got
    return block


def on_device(normal_matrix, right_sides):
    row_blocks, _, block, col_blocks, _, _ = normal_matrix.shape
    col_id = lax.axis_index("col")
    row_id = lax.axis_index("row")
    col_count = lax.axis_size("col")
    row_count = lax.axis_size("row")
    side_count = right_sides.shape[0]
    local = normal_matrix.reshape(row_blocks * block, col_blocks * block)

    left = spread(local[:, :block], "col")
    top = jnp.concatenate([local[:block], right_sides[:, 0, 0, :].T], axis=1)
    top = spread_wide(top, "row")
    corner_raw = spread_wide(top[:, :block], "col")

    corner = jnp.linalg.cholesky(corner_raw)
    rhs = jnp.concatenate([left.T, top], axis=1)
    solved = jax.scipy.linalg.solve_triangular(corner, rhs, lower=True).T
    rows_factor = solved[: row_blocks * block]
    cols_factor = solved[row_blocks * block: (row_blocks + col_blocks) * block]
    lead = solved[(row_blocks + col_blocks) * block:]

    change = jnp.dot(
        rows_factor,
        cols_factor.T,
        precision=lax.Precision.HIGHEST,
        preferred_element_type=jnp.float32,
    )
    trailing = (local - change).reshape(row_blocks, block, col_blocks, block)
    global_rows = row_id + row_count * jnp.arange(row_blocks, dtype=jnp.int32)
    global_cols = col_id + col_count * jnp.arange(col_blocks, dtype=jnp.int32)
    inner = (global_rows[:, None, None, None] >= 1) & (global_cols[None, None, :, None] >= 1)
    result = jnp.where(inner, trailing, jnp.float32(0.0))
    column = jnp.where(
        global_rows[:, None, None] == 0, corner[None], rows_factor.reshape(row_blocks, block, block)
    )
    result = jnp.where((global_cols == 0)[None, None, :, None], column[:, :, None, :], result)
    result = result.reshape(normal_matrix.shape)

    flat = right_sides.reshape(side_count, row_blocks * block)
    reduced = flat - jnp.dot(
        lead, rows_factor.T, precision=lax.Precision.HIGHEST, preferred_element_type=jnp.float32
    )
    reduced = reduced.reshape(side_count, row_blocks, block)
    reduced = jnp.where((global_rows == 0)[None, :, None], lead[:, None, :], reduced)
    return (result, reduced.reshape(right_sides.shape))


def solution(mesh):
    placed = (P(None, "row", None, None, "col", None), P("col", None, "row", None))
    return jax.shard_map(
        on_device,
        mesh=mesh,
        in_specs=placed,
        out_specs=(P(None, "row", None, None, "col", None), P("col", None, "row", None)),
        check_vma=False,
    )
```

```python
import jax
import jax.numpy as jnp
from jax import lax
from jax.sharding import PartitionSpec as P


def tree(block, axis, wide):
    count = lax.axis_size(axis)
    index = lax.axis_index(axis)
    radices = []
    rest = count
    while rest > 1:
        radix = (4 if rest % 4 == 0 else rest) if wide else 2
        radices.append(radix)
        rest //= radix
    span = count
    for radix in radices:
        span //= radix
        got = block
        for digit in range(1, radix):
            pairs = [
                (i, i + digit * span)
                for i in range(0, count, span * radix)
                if i + digit * span < count
            ]
            arrived = lax.ppermute(block, axis, pairs)
            mine = (index % (span * radix)) == digit * span
            got = jnp.where(mine, arrived, got)
        block = yield got
    return block


def lockstep(*trees):
    held = [None] * len(trees)
    results = [None] * len(trees)
    live = []
    for k, t in enumerate(trees):
        try:
            held[k] = next(t)
            live.append(k)
        except StopIteration as stop:
            results[k] = stop.value
    while live:
        tied = lax.optimization_barrier(tuple(held[k] for k in live))
        still = []
        for k, value in zip(live, tied):
            try:
                held[k] = trees[k].send(value)
                still.append(k)
            except StopIteration as stop:
                results[k] = stop.value
        live = still
    return results


def pause(gen, rounds):
    got = next(gen)
    for step in range(rounds):
        tied = yield got
        if step < rounds - 1:
            got = gen.send(tied)
    return tied, gen


def resume(paused):
    value, gen = paused
    try:
        got = gen.send(value)
        while True:
            tied = yield got
            got = gen.send(tied)
    except StopIteration as stop:
        return stop.value


def on_device(normal_matrix, right_sides):
    row_blocks, _, block, col_blocks, _, _ = normal_matrix.shape
    col_id = lax.axis_index("col")
    row_id = lax.axis_index("row")
    col_count = lax.axis_size("col")
    row_count = lax.axis_size("row")
    side_count = right_sides.shape[0]
    local = normal_matrix.reshape(row_blocks * block, col_blocks * block)

    top = jnp.concatenate([local[:block], right_sides[:, 0, 0, :].T], axis=1)
    row_tree = tree(top, "row", True)
    col_tree = tree(local[:, :block], "col", False)
    top, paused = lockstep(row_tree, pause(col_tree, 2))
    corner_raw, left = lockstep(tree(top[:, :block], "col", True), resume(paused))

    corner = jnp.linalg.cholesky(corner_raw)
    rhs = jnp.concatenate([left.T, top], axis=1)
    solved = jax.scipy.linalg.solve_triangular(corner, rhs, lower=True).T
    rows_factor = solved[: row_blocks * block]
    cols_factor = solved[row_blocks * block: (row_blocks + col_blocks) * block]
    lead = solved[(row_blocks + col_blocks) * block:]

    change = jnp.dot(
        rows_factor,
        cols_factor.T,
        precision=lax.Precision.HIGHEST,
        preferred_element_type=jnp.float32,
    )
    trailing = (local - change).reshape(row_blocks, block, col_blocks, block)
    global_rows = row_id + row_count * jnp.arange(row_blocks, dtype=jnp.int32)
    global_cols = col_id + col_count * jnp.arange(col_blocks, dtype=jnp.int32)
    inner = (global_rows[:, None, None, None] >= 1) & (global_cols[None, None, :, None] >= 1)
    result = jnp.where(inner, trailing, jnp.float32(0.0))
    column = jnp.where(
        global_rows[:, None, None] == 0, corner[None], rows_factor.reshape(row_blocks, block, block)
    )
    result = jnp.where((global_cols == 0)[None, None, :, None], column[:, :, None, :], result)
    result = result.reshape(normal_matrix.shape)

    flat = right_sides.reshape(side_count, row_blocks * block)
    reduced = flat - jnp.dot(
        lead, rows_factor.T, precision=lax.Precision.HIGHEST, preferred_element_type=jnp.float32
    )
    reduced = reduced.reshape(side_count, row_blocks, block)
    reduced = jnp.where((global_rows == 0)[None, :, None], lead[:, None, :], reduced)
    return (result, reduced.reshape(right_sides.shape))


def solution(mesh):
    placed = (P(None, "row", None, None, "col", None), P("col", None, "row", None))
    return jax.shard_map(
        on_device,
        mesh=mesh,
        in_specs=placed,
        out_specs=(P(None, "row", None, None, "col", None), P("col", None, "row", None)),
        check_vma=False,
    )
```

```python
import jax
import jax.numpy as jnp
from jax import lax
from jax.sharding import PartitionSpec as P


def spread(block, axis):
    count = lax.axis_size(axis)
    index = lax.axis_index(axis)
    step = 1
    while 2 * step < count:
        step *= 2
    while step >= 1:
        pairs = [(i, i + step) for i in range(0, count, 2 * step) if i + step < count]
        arrived = lax.ppermute(block, axis, pairs)
        block = jnp.where(index % (2 * step) == step, arrived, block)
        step //= 2
    return block


def spread_wide(block, axis):
    count = lax.axis_size(axis)
    index = lax.axis_index(axis)
    radices = []
    rest = count
    while rest > 1:
        radix = 4 if rest % 4 == 0 else rest
        radices.append(radix)
        rest //= radix
    span = count
    for radix in radices:
        span //= radix
        got = block
        for digit in range(1, radix):
            pairs = [(i, i + digit * span) for i in range(0, count, span * radix)]
            arrived = lax.ppermute(block, axis, pairs)
            mine = (index % (span * radix)) == digit * span
            got = jnp.where(mine, arrived, got)
        block = got
    return block


def on_device(normal_matrix, right_sides):
    row_blocks, _, block, col_blocks, _, _ = normal_matrix.shape
    col_id = lax.axis_index("col")
    row_id = lax.axis_index("row")
    col_count = lax.axis_size("col")
    row_count = lax.axis_size("row")
    side_count = right_sides.shape[0]
    local = normal_matrix.reshape(row_blocks * block, col_blocks * block)
    identity = jnp.eye(block, dtype=jnp.float32)

    def factor(corner_raw):
        corner = jnp.linalg.cholesky(corner_raw)
        inverse = jax.scipy.linalg.solve_triangular(corner, identity, lower=True)
        return corner, inverse

    def skip(corner_raw):
        return jnp.zeros_like(corner_raw), jnp.zeros_like(corner_raw)

    holder = (row_id == 0) & (col_id == 0)
    corner, inverse = lax.cond(holder, factor, skip, local[:block, :block])
    inverse = spread_wide(spread_wide(inverse, "row"), "col")
    left = spread(local[:, :block], "col")
    top = jnp.concatenate([local[:block], right_sides[:, 0, 0, :].T], axis=1)
    top = spread_wide(top, "row")

    rows_factor = jnp.dot(
        left, inverse.T, precision=lax.Precision.HIGHEST, preferred_element_type=jnp.float32
    )
    solved = jnp.dot(
        inverse, top, precision=lax.Precision.HIGHEST, preferred_element_type=jnp.float32
    ).T
    cols_factor = solved[: col_blocks * block]
    lead = solved[col_blocks * block:]

    change = jnp.dot(
        rows_factor,
        cols_factor.T,
        precision=lax.Precision.HIGHEST,
        preferred_element_type=jnp.float32,
    )
    trailing = (local - change).reshape(row_blocks, block, col_blocks, block)
    global_rows = row_id + row_count * jnp.arange(row_blocks, dtype=jnp.int32)
    global_cols = col_id + col_count * jnp.arange(col_blocks, dtype=jnp.int32)
    inner = (global_rows[:, None, None, None] >= 1) & (global_cols[None, None, :, None] >= 1)
    result = jnp.where(inner, trailing, jnp.float32(0.0))
    column = jnp.where(
        global_rows[:, None, None] == 0, corner[None], rows_factor.reshape(row_blocks, block, block)
    )
    result = jnp.where((global_cols == 0)[None, None, :, None], column[:, :, None, :], result)
    result = result.reshape(normal_matrix.shape)

    flat = right_sides.reshape(side_count, row_blocks * block)
    reduced = flat - jnp.dot(
        lead, rows_factor.T, precision=lax.Precision.HIGHEST, preferred_element_type=jnp.float32
    )
    reduced = reduced.reshape(side_count, row_blocks, block)
    reduced = jnp.where((global_rows == 0)[None, :, None], lead[:, None, :], reduced)
    return (result, reduced.reshape(right_sides.shape))


def solution(mesh):
    placed = (P(None, "row", None, None, "col", None), P("col", None, "row", None))
    return jax.shard_map(
        on_device,
        mesh=mesh,
        in_specs=placed,
        out_specs=(P(None, "row", None, None, "col", None), P("col", None, "row", None)),
        check_vma=False,
    )
```

```python
import jax
import jax.numpy as jnp
from jax import lax
from jax.sharding import PartitionSpec as P


def spread(block, axis):
    count = lax.axis_size(axis)
    index = lax.axis_index(axis)
    step = 1
    while 2 * step < count:
        step *= 2
    while step >= 1:
        pairs = [(i, i + step) for i in range(0, count, 2 * step) if i + step < count]
        arrived = lax.ppermute(block, axis, pairs)
        block = jnp.where(index % (2 * step) == step, arrived, block)
        step //= 2
    return block


def spread_wide(block, axis, root=0):
    count = lax.axis_size(axis)
    index = lax.axis_index(axis) ^ root
    radices = []
    rest = count
    while rest > 1:
        radix = 4 if rest % 4 == 0 else rest
        radices.append(radix)
        rest //= radix
    span = count
    for radix in radices:
        span //= radix
        got = block
        for digit in range(1, radix):
            pairs = [
                (i ^ root, (i + digit * span) ^ root)
                for i in range(0, count, span * radix)
            ]
            arrived = lax.ppermute(block, axis, pairs)
            mine = (index % (span * radix)) == digit * span
            got = jnp.where(mine, arrived, got)
        block = got
    return block


def on_device(normal_matrix, right_sides):
    row_blocks, _, block, col_blocks, _, _ = normal_matrix.shape
    col_id = lax.axis_index("col")
    row_id = lax.axis_index("row")
    col_count = lax.axis_size("col")
    row_count = lax.axis_size("row")
    side_count = right_sides.shape[0]
    local = normal_matrix.reshape(row_blocks * block, col_blocks * block)
    identity = jnp.eye(block, dtype=jnp.float32)

    def factor(corner_raw):
        corner = jnp.linalg.cholesky(corner_raw)
        inverse = jax.scipy.linalg.solve_triangular(corner, identity, lower=True)
        return corner, inverse

    def skip(corner_raw):
        return jnp.zeros_like(corner_raw), jnp.zeros_like(corner_raw)

    corner_raw = lax.ppermute(local[:block, :block], "col", [(0, 1)])
    holder = (row_id == 0) & (col_id == 1)
    corner, inverse = lax.cond(holder, factor, skip, corner_raw)
    corner = lax.ppermute(corner, "col", [(1, 0)])
    inverse = spread_wide(spread_wide(inverse, "row"), "col", root=1)
    left = spread(local[:, :block], "col")
    top = jnp.concatenate([local[:block], right_sides[:, 0, 0, :].T], axis=1)
    top = spread_wide(top, "row")

    rows_factor = jnp.dot(
        left, inverse.T, precision=lax.Precision.HIGHEST, preferred_element_type=jnp.float32
    )
    solved = jnp.dot(
        inverse, top, precision=lax.Precision.HIGHEST, preferred_element_type=jnp.float32
    ).T
    cols_factor = solved[: col_blocks * block]
    lead = solved[col_blocks * block:]

    change = jnp.dot(
        rows_factor,
        cols_factor.T,
        precision=lax.Precision.HIGHEST,
        preferred_element_type=jnp.float32,
    )
    trailing = (local - change).reshape(row_blocks, block, col_blocks, block)
    global_rows = row_id + row_count * jnp.arange(row_blocks, dtype=jnp.int32)
    global_cols = col_id + col_count * jnp.arange(col_blocks, dtype=jnp.int32)
    inner = (global_rows[:, None, None, None] >= 1) & (global_cols[None, None, :, None] >= 1)
    result = jnp.where(inner, trailing, jnp.float32(0.0))
    column = jnp.where(
        global_rows[:, None, None] == 0, corner[None], rows_factor.reshape(row_blocks, block, block)
    )
    result = jnp.where((global_cols == 0)[None, None, :, None], column[:, :, None, :], result)
    result = result.reshape(normal_matrix.shape)

    flat = right_sides.reshape(side_count, row_blocks * block)
    reduced = flat - jnp.dot(
        lead, rows_factor.T, precision=lax.Precision.HIGHEST, preferred_element_type=jnp.float32
    )
    reduced = reduced.reshape(side_count, row_blocks, block)
    reduced = jnp.where((global_rows == 0)[None, :, None], lead[:, None, :], reduced)
    return (result, reduced.reshape(right_sides.shape))


def solution(mesh):
    placed = (P(None, "row", None, None, "col", None), P("col", None, "row", None))
    return jax.shard_map(
        on_device,
        mesh=mesh,
        in_specs=placed,
        out_specs=(P(None, "row", None, None, "col", None), P("col", None, "row", None)),
        check_vma=False,
    )
```

```python
import jax
import jax.numpy as jnp
from jax import lax
from jax.sharding import PartitionSpec as P


def spread(block, axis):
    count = lax.axis_size(axis)
    index = lax.axis_index(axis)
    step = 1
    while 2 * step < count:
        step *= 2
    while step >= 1:
        pairs = [(i, i + step) for i in range(0, count, 2 * step) if i + step < count]
        arrived = lax.ppermute(block, axis, pairs)
        block = jnp.where(index % (2 * step) == step, arrived, block)
        step //= 2
    return block


def spread_wide(block, axis):
    count = lax.axis_size(axis)
    index = lax.axis_index(axis)
    radices = []
    rest = count
    while rest > 1:
        radix = 4 if rest % 4 == 0 else rest
        radices.append(radix)
        rest //= radix
    span = count
    for radix in radices:
        span //= radix
        got = block
        for digit in range(1, radix):
            pairs = [(i, i + digit * span) for i in range(0, count, span * radix)]
            arrived = lax.ppermute(block, axis, pairs)
            mine = (index % (span * radix)) == digit * span
            got = jnp.where(mine, arrived, got)
        block = got
    return block


def on_device(normal_matrix, right_sides):
    row_blocks, _, block, col_blocks, _, _ = normal_matrix.shape
    col_id = lax.axis_index("col")
    row_id = lax.axis_index("row")
    col_count = lax.axis_size("col")
    row_count = lax.axis_size("row")
    side_count = right_sides.shape[0]
    local = normal_matrix.reshape(row_blocks * block, col_blocks * block)
    identity = jnp.eye(block, dtype=jnp.float32)

    def factor(corner_raw):
        corner = jnp.linalg.cholesky(corner_raw)
        inverse = jax.scipy.linalg.solve_triangular(corner, identity, lower=True)
        return corner, inverse

    def skip(corner_raw):
        return jnp.zeros_like(corner_raw), jnp.zeros_like(corner_raw)

    holder = (row_id == 0) & (col_id == 0)
    corner, inverse = lax.cond(holder, factor, skip, local[:block, :block])
    top = jnp.concatenate([local[:block], right_sides[:, 0, 0, :].T, inverse], axis=1)
    top = spread_wide(top, "row")
    width = col_blocks * block + side_count
    left = jnp.concatenate([local[:, :block], top[:, width:]], axis=0)
    left = spread_wide(left, "col")
    inverse = left[row_blocks * block:]
    left = left[: row_blocks * block]
    top = top[:, :width]

    rows_factor = jnp.dot(
        left, inverse.T, precision=lax.Precision.HIGHEST, preferred_element_type=jnp.float32
    )
    solved = jnp.dot(
        inverse, top, precision=lax.Precision.HIGHEST, preferred_element_type=jnp.float32
    ).T
    cols_factor = solved[: col_blocks * block]
    lead = solved[col_blocks * block:]

    change = jnp.dot(
        rows_factor,
        cols_factor.T,
        precision=lax.Precision.HIGHEST,
        preferred_element_type=jnp.float32,
    )
    trailing = (local - change).reshape(row_blocks, block, col_blocks, block)
    global_rows = row_id + row_count * jnp.arange(row_blocks, dtype=jnp.int32)
    global_cols = col_id + col_count * jnp.arange(col_blocks, dtype=jnp.int32)
    inner = (global_rows[:, None, None, None] >= 1) & (global_cols[None, None, :, None] >= 1)
    result = jnp.where(inner, trailing, jnp.float32(0.0))
    column = jnp.where(
        global_rows[:, None, None] == 0, corner[None], rows_factor.reshape(row_blocks, block, block)
    )
    result = jnp.where((global_cols == 0)[None, None, :, None], column[:, :, None, :], result)
    result = result.reshape(normal_matrix.shape)

    flat = right_sides.reshape(side_count, row_blocks * block)
    reduced = flat - jnp.dot(
        lead, rows_factor.T, precision=lax.Precision.HIGHEST, preferred_element_type=jnp.float32
    )
    reduced = reduced.reshape(side_count, row_blocks, block)
    reduced = jnp.where((global_rows == 0)[None, :, None], lead[:, None, :], reduced)
    return (result, reduced.reshape(right_sides.shape))


def solution(mesh):
    placed = (P(None, "row", None, None, "col", None), P("col", None, "row", None))
    return jax.shard_map(
        on_device,
        mesh=mesh,
        in_specs=placed,
        out_specs=(P(None, "row", None, None, "col", None), P("col", None, "row", None)),
        check_vma=False,
    )
```

```python
import jax
import jax.numpy as jnp
from jax import lax
from jax.experimental import pallas as pl
from jax.sharding import PartitionSpec as P


def spread(block, axis):
    count = lax.axis_size(axis)
    index = lax.axis_index(axis)
    step = 1
    while 2 * step < count:
        step *= 2
    while step >= 1:
        pairs = [(i, i + step) for i in range(0, count, 2 * step) if i + step < count]
        arrived = lax.ppermute(block, axis, pairs)
        block = jnp.where(index % (2 * step) == step, arrived, block)
        step //= 2
    return block


def spread_wide(block, axis):
    count = lax.axis_size(axis)
    index = lax.axis_index(axis)
    radices = []
    rest = count
    while rest > 1:
        radix = 4 if rest % 4 == 0 else rest
        radices.append(radix)
        rest //= radix
    span = count
    for radix in radices:
        span //= radix
        got = block
        for digit in range(1, radix):
            pairs = [(i, i + digit * span) for i in range(0, count, span * radix)]
            arrived = lax.ppermute(block, axis, pairs)
            mine = (index % (span * radix)) == digit * span
            got = jnp.where(mine, arrived, got)
        block = got
    return block


def _factor_kernel(block_ref, factor_ref, inverse_ref):
    n = block_ref.shape[0]
    rows = lax.broadcasted_iota(jnp.int32, (n, n), 0)
    cols = lax.broadcasted_iota(jnp.int32, (n, n), 1)
    upper = block_ref[...]
    lower = jnp.where(rows == cols, jnp.float32(1.0), jnp.float32(0.0))
    index = lax.broadcasted_iota(jnp.int32, (n, 1), 0)
    for k in range(n):
        pivot_upper = upper[k:k + 1, :]
        pivot_lower = lower[k:k + 1, :]
        scale = jnp.where(
            index > k, upper[:, k:k + 1] / pivot_upper[:, k:k + 1], jnp.float32(0.0)
        )
        upper = upper - scale * pivot_upper
        lower = lower - scale * pivot_lower
    diagonal = jnp.sum(jnp.where(rows == cols, upper, 0.0), axis=1, keepdims=True)
    root = jnp.sqrt(diagonal)
    factor_ref[...] = jnp.where(rows <= cols, upper, 0.0) / root
    inverse_ref[...] = lower / root


def factor_and_invert(block):
    n = block.shape[0]
    return pl.pallas_call(
        _factor_kernel,
        out_shape=(
            jax.ShapeDtypeStruct((n, n), jnp.float32),
            jax.ShapeDtypeStruct((n, n), jnp.float32),
        ),
    )(block)


def on_device(normal_matrix, right_sides):
    row_blocks, _, block, col_blocks, _, _ = normal_matrix.shape
    col_id = lax.axis_index("col")
    row_id = lax.axis_index("row")
    col_count = lax.axis_size("col")
    row_count = lax.axis_size("row")
    side_count = right_sides.shape[0]
    local = normal_matrix.reshape(row_blocks * block, col_blocks * block)

    def factor(corner_raw):
        corner_t, inverse = factor_and_invert(corner_raw)
        return corner_t.T, inverse

    def skip(corner_raw):
        return jnp.zeros_like(corner_raw), jnp.zeros_like(corner_raw)

    holder = (row_id == 0) & (col_id == 0)
    corner, inverse = lax.cond(holder, factor, skip, local[:block, :block])
    inverse = spread_wide(spread_wide(inverse, "row"), "col")
    left = spread(local[:, :block], "col")
    top = jnp.concatenate([local[:block], right_sides[:, 0, 0, :].T], axis=1)
    top = spread_wide(top, "row")

    rows_factor = jnp.dot(
        left, inverse.T, precision=lax.Precision.HIGHEST, preferred_element_type=jnp.float32
    )
    solved = jnp.dot(
        inverse, top, precision=lax.Precision.HIGHEST, preferred_element_type=jnp.float32
    ).T
    cols_factor = solved[: col_blocks * block]
    lead = solved[col_blocks * block:]

    change = jnp.dot(
        rows_factor,
        cols_factor.T,
        precision=lax.Precision.HIGHEST,
        preferred_element_type=jnp.float32,
    )
    trailing = (local - change).reshape(row_blocks, block, col_blocks, block)
    global_rows = row_id + row_count * jnp.arange(row_blocks, dtype=jnp.int32)
    global_cols = col_id + col_count * jnp.arange(col_blocks, dtype=jnp.int32)
    inner = (global_rows[:, None, None, None] >= 1) & (global_cols[None, None, :, None] >= 1)
    result = jnp.where(inner, trailing, jnp.float32(0.0))
    column = jnp.where(
        global_rows[:, None, None] == 0, corner[None], rows_factor.reshape(row_blocks, block, block)
    )
    result = jnp.where((global_cols == 0)[None, None, :, None], column[:, :, None, :], result)
    result = result.reshape(normal_matrix.shape)

    flat = right_sides.reshape(side_count, row_blocks * block)
    reduced = flat - jnp.dot(
        lead, rows_factor.T, precision=lax.Precision.HIGHEST, preferred_element_type=jnp.float32
    )
    reduced = reduced.reshape(side_count, row_blocks, block)
    reduced = jnp.where((global_rows == 0)[None, :, None], lead[:, None, :], reduced)
    return (result, reduced.reshape(right_sides.shape))


def solution(mesh):
    placed = (P(None, "row", None, None, "col", None), P("col", None, "row", None))
    return jax.shard_map(
        on_device,
        mesh=mesh,
        in_specs=placed,
        out_specs=(P(None, "row", None, None, "col", None), P("col", None, "row", None)),
        check_vma=False,
    )
```

```python
import jax
import jax.numpy as jnp
from jax import lax
from jax.experimental import pallas as pl
from jax.sharding import PartitionSpec as P


def spread(block, axis):
    count = lax.axis_size(axis)
    index = lax.axis_index(axis)
    step = 1
    while 2 * step < count:
        step *= 2
    while step >= 1:
        pairs = [(i, i + step) for i in range(0, count, 2 * step) if i + step < count]
        arrived = lax.ppermute(block, axis, pairs)
        block = jnp.where(index % (2 * step) == step, arrived, block)
        step //= 2
    return block


def spread_wide(block, axis):
    count = lax.axis_size(axis)
    index = lax.axis_index(axis)
    radices = []
    rest = count
    while rest > 1:
        radix = 4 if rest % 4 == 0 else rest
        radices.append(radix)
        rest //= radix
    span = count
    for radix in radices:
        span //= radix
        got = block
        for digit in range(1, radix):
            pairs = [(i, i + digit * span) for i in range(0, count, span * radix)]
            arrived = lax.ppermute(block, axis, pairs)
            mine = (index % (span * radix)) == digit * span
            got = jnp.where(mine, arrived, got)
        block = got
    return block


def _factor_kernel(block_ref, factor_ref, inverse_ref):
    n = block_ref.shape[0]
    tile = 8
    upper = [block_ref[t * tile:(t + 1) * tile, :] for t in range(n // tile)]
    tile_rows = lax.broadcasted_iota(jnp.int32, (tile, n), 0)
    tile_cols = lax.broadcasted_iota(jnp.int32, (tile, n), 1)
    lower = [
        jnp.where(tile_rows + t * tile == tile_cols, jnp.float32(1.0), jnp.float32(0.0))
        for t in range(n // tile)
    ]
    index = lax.broadcasted_iota(jnp.int32, (tile, 1), 0)
    for k in range(n):
        first = k // tile
        pivot_upper = upper[first][k % tile:k % tile + 1, :]
        pivot_lower = lower[first][k % tile:k % tile + 1, :]
        reciprocal = 1.0 / pivot_upper[:, k:k + 1]
        for t in range(first, n // tile):
            scale = upper[t][:, k:k + 1] * reciprocal
            if t == first:
                scale = jnp.where(index + t * tile > k, scale, jnp.float32(0.0))
            upper[t] = upper[t] - scale * pivot_upper
            lower[t] = lower[t] - scale * pivot_lower
    upper = jnp.concatenate(upper, axis=0)
    lower = jnp.concatenate(lower, axis=0)
    rows = lax.broadcasted_iota(jnp.int32, (n, n), 0)
    cols = lax.broadcasted_iota(jnp.int32, (n, n), 1)
    diagonal = jnp.sum(jnp.where(rows == cols, upper, 0.0), axis=1, keepdims=True)
    root = jnp.sqrt(diagonal)
    factor_ref[...] = jnp.where(rows <= cols, upper, 0.0) / root
    inverse_ref[...] = lower / root


def factor_and_invert(block):
    n = block.shape[0]
    return pl.pallas_call(
        _factor_kernel,
        out_shape=(
            jax.ShapeDtypeStruct((n, n), jnp.float32),
            jax.ShapeDtypeStruct((n, n), jnp.float32),
        ),
    )(block)


def on_device(normal_matrix, right_sides):
    row_blocks, _, block, col_blocks, _, _ = normal_matrix.shape
    col_id = lax.axis_index("col")
    row_id = lax.axis_index("row")
    col_count = lax.axis_size("col")
    row_count = lax.axis_size("row")
    side_count = right_sides.shape[0]
    local = normal_matrix.reshape(row_blocks * block, col_blocks * block)

    def factor(corner_raw):
        corner_t, inverse = factor_and_invert(corner_raw)
        return corner_t.T, inverse

    def skip(corner_raw):
        return jnp.zeros_like(corner_raw), jnp.zeros_like(corner_raw)

    holder = (row_id == 0) & (col_id == 0)
    corner, inverse = lax.cond(holder, factor, skip, local[:block, :block])
    inverse = spread_wide(spread_wide(inverse, "row"), "col")
    left = spread(local[:, :block], "col")
    top = jnp.concatenate([local[:block], right_sides[:, 0, 0, :].T], axis=1)
    top = spread_wide(top, "row")

    rows_factor = jnp.dot(
        left, inverse.T, precision=lax.Precision.HIGHEST, preferred_element_type=jnp.float32
    )
    solved = jnp.dot(
        inverse, top, precision=lax.Precision.HIGHEST, preferred_element_type=jnp.float32
    ).T
    cols_factor = solved[: col_blocks * block]
    lead = solved[col_blocks * block:]

    change = jnp.dot(
        rows_factor,
        cols_factor.T,
        precision=lax.Precision.HIGHEST,
        preferred_element_type=jnp.float32,
    )
    trailing = (local - change).reshape(row_blocks, block, col_blocks, block)
    global_rows = row_id + row_count * jnp.arange(row_blocks, dtype=jnp.int32)
    global_cols = col_id + col_count * jnp.arange(col_blocks, dtype=jnp.int32)
    inner = (global_rows[:, None, None, None] >= 1) & (global_cols[None, None, :, None] >= 1)
    result = jnp.where(inner, trailing, jnp.float32(0.0))
    column = jnp.where(
        global_rows[:, None, None] == 0, corner[None], rows_factor.reshape(row_blocks, block, block)
    )
    result = jnp.where((global_cols == 0)[None, None, :, None], column[:, :, None, :], result)
    result = result.reshape(normal_matrix.shape)

    flat = right_sides.reshape(side_count, row_blocks * block)
    reduced = flat - jnp.dot(
        lead, rows_factor.T, precision=lax.Precision.HIGHEST, preferred_element_type=jnp.float32
    )
    reduced = reduced.reshape(side_count, row_blocks, block)
    reduced = jnp.where((global_rows == 0)[None, :, None], lead[:, None, :], reduced)
    return (result, reduced.reshape(right_sides.shape))


def solution(mesh):
    placed = (P(None, "row", None, None, "col", None), P("col", None, "row", None))
    return jax.shard_map(
        on_device,
        mesh=mesh,
        in_specs=placed,
        out_specs=(P(None, "row", None, None, "col", None), P("col", None, "row", None)),
        check_vma=False,
    )
```

```python
import jax
import jax.numpy as jnp
from jax import lax
from jax.experimental import pallas as pl
from jax.sharding import PartitionSpec as P


def spread(block, axis):
    count = lax.axis_size(axis)
    index = lax.axis_index(axis)
    step = 1
    while 2 * step < count:
        step *= 2
    while step >= 1:
        pairs = [(i, i + step) for i in range(0, count, 2 * step) if i + step < count]
        arrived = lax.ppermute(block, axis, pairs)
        block = jnp.where(index % (2 * step) == step, arrived, block)
        step //= 2
    return block


def spread_wide(block, axis):
    count = lax.axis_size(axis)
    index = lax.axis_index(axis)
    radices = []
    rest = count
    while rest > 1:
        radix = 4 if rest % 4 == 0 else rest
        radices.append(radix)
        rest //= radix
    span = count
    for radix in radices:
        span //= radix
        got = block
        for digit in range(1, radix):
            pairs = [(i, i + digit * span) for i in range(0, count, span * radix)]
            arrived = lax.ppermute(block, axis, pairs)
            mine = (index % (span * radix)) == digit * span
            got = jnp.where(mine, arrived, got)
        block = got
    return block


def _factor_kernel(block_ref, factor_ref, inverse_ref):
    n = block_ref.shape[0]
    tile = 8
    upper = [block_ref[t * tile:(t + 1) * tile, :] for t in range(n // tile)]
    tile_rows = lax.broadcasted_iota(jnp.int32, (tile, n), 0)
    tile_cols = lax.broadcasted_iota(jnp.int32, (tile, n), 1)
    lower = [
        jnp.where(tile_rows + t * tile == tile_cols, jnp.float32(1.0), jnp.float32(0.0))
        for t in range(n // tile)
    ]
    index = lax.broadcasted_iota(jnp.int32, (tile, 1), 0)
    for k in range(n):
        first = k // tile
        pivot_upper = upper[first][k % tile:k % tile + 1, :]
        pivot_lower = lower[first][k % tile:k % tile + 1, :]
        reciprocal = 1.0 / pivot_upper[:, k:k + 1]
        for t in range(first, n // tile):
            scale = upper[t][:, k:k + 1] * reciprocal
            if t == first:
                scale = jnp.where(index + t * tile > k, scale, jnp.float32(0.0))
            upper[t] = upper[t] - scale * pivot_upper
            lower[t] = lower[t] - scale * pivot_lower
    upper = jnp.concatenate(upper, axis=0)
    lower = jnp.concatenate(lower, axis=0)
    rows = lax.broadcasted_iota(jnp.int32, (n, n), 0)
    cols = lax.broadcasted_iota(jnp.int32, (n, n), 1)
    diagonal = jnp.sum(jnp.where(rows == cols, upper, 0.0), axis=1, keepdims=True)
    root = jnp.sqrt(diagonal)
    factor_ref[...] = jnp.where(rows <= cols, upper, 0.0) / root
    inverse_ref[...] = lower / root


def factor_and_invert(block):
    n = block.shape[0]
    return pl.pallas_call(
        _factor_kernel,
        out_shape=(
            jax.ShapeDtypeStruct((n, n), jnp.float32),
            jax.ShapeDtypeStruct((n, n), jnp.float32),
        ),
    )(block)


def on_device(normal_matrix, right_sides):
    row_blocks, _, block, col_blocks, _, _ = normal_matrix.shape
    col_id = lax.axis_index("col")
    row_id = lax.axis_index("row")
    col_count = lax.axis_size("col")
    row_count = lax.axis_size("row")
    side_count = right_sides.shape[0]
    local = normal_matrix.reshape(row_blocks * block, col_blocks * block)

    def factor(corner_raw):
        corner_t, inverse = factor_and_invert(corner_raw)
        return corner_t.T, inverse

    def skip(corner_raw):
        return jnp.zeros_like(corner_raw), jnp.zeros_like(corner_raw)

    holder = (row_id == 0) & (col_id == 0)
    corner, inverse = lax.cond(holder, factor, skip, local[:block, :block])
    left = spread(local[:, :block], "col")
    width = col_blocks * block + side_count
    top = jnp.concatenate([local[:block], right_sides[:, 0, 0, :].T, inverse], axis=1)
    top = spread_wide(top, "row")
    inverse = spread_wide(top[:, width:], "col")
    top = top[:, :width]

    rows_factor = jnp.dot(
        left, inverse.T, precision=lax.Precision.HIGHEST, preferred_element_type=jnp.float32
    )
    solved = jnp.dot(
        inverse, top, precision=lax.Precision.HIGHEST, preferred_element_type=jnp.float32
    ).T
    cols_factor = solved[: col_blocks * block]
    lead = solved[col_blocks * block:]

    change = jnp.dot(
        rows_factor,
        cols_factor.T,
        precision=lax.Precision.HIGHEST,
        preferred_element_type=jnp.float32,
    )
    trailing = (local - change).reshape(row_blocks, block, col_blocks, block)
    global_rows = row_id + row_count * jnp.arange(row_blocks, dtype=jnp.int32)
    global_cols = col_id + col_count * jnp.arange(col_blocks, dtype=jnp.int32)
    inner = (global_rows[:, None, None, None] >= 1) & (global_cols[None, None, :, None] >= 1)
    result = jnp.where(inner, trailing, jnp.float32(0.0))
    column = jnp.where(
        global_rows[:, None, None] == 0, corner[None], rows_factor.reshape(row_blocks, block, block)
    )
    result = jnp.where((global_cols == 0)[None, None, :, None], column[:, :, None, :], result)
    result = result.reshape(normal_matrix.shape)

    flat = right_sides.reshape(side_count, row_blocks * block)
    reduced = flat - jnp.dot(
        lead, rows_factor.T, precision=lax.Precision.HIGHEST, preferred_element_type=jnp.float32
    )
    reduced = reduced.reshape(side_count, row_blocks, block)
    reduced = jnp.where((global_rows == 0)[None, :, None], lead[:, None, :], reduced)
    return (result, reduced.reshape(right_sides.shape))


def solution(mesh):
    placed = (P(None, "row", None, None, "col", None), P("col", None, "row", None))
    return jax.shard_map(
        on_device,
        mesh=mesh,
        in_specs=placed,
        out_specs=(P(None, "row", None, None, "col", None), P("col", None, "row", None)),
        check_vma=False,
    )
```

```python
import jax
import jax.numpy as jnp
from jax import lax
from jax.experimental import pallas as pl
from jax.sharding import PartitionSpec as P


def spread(block, axis):
    count = lax.axis_size(axis)
    index = lax.axis_index(axis)
    step = 1
    while 2 * step < count:
        step *= 2
    while step >= 1:
        pairs = [(i, i + step) for i in range(0, count, 2 * step) if i + step < count]
        arrived = lax.ppermute(block, axis, pairs)
        block = jnp.where(index % (2 * step) == step, arrived, block)
        step //= 2
    return block


def spread_wide(block, axis):
    count = lax.axis_size(axis)
    index = lax.axis_index(axis)
    radices = []
    rest = count
    while rest > 1:
        radix = 4 if rest % 4 == 0 else rest
        radices.append(radix)
        rest //= radix
    span = count
    for radix in radices:
        span //= radix
        got = block
        for digit in range(1, radix):
            pairs = [(i, i + digit * span) for i in range(0, count, span * radix)]
            arrived = lax.ppermute(block, axis, pairs)
            mine = (index % (span * radix)) == digit * span
            got = jnp.where(mine, arrived, got)
        block = got
    return block


def _factor_kernel(block_ref, factor_ref, inverse_ref):
    n = block_ref.shape[0]
    tile = 8
    upper = [block_ref[t * tile:(t + 1) * tile, :] for t in range(n // tile)]
    tile_rows = lax.broadcasted_iota(jnp.int32, (tile, n), 0)
    tile_cols = lax.broadcasted_iota(jnp.int32, (tile, n), 1)
    lower = [
        jnp.where(tile_rows + t * tile == tile_cols, jnp.float32(1.0), jnp.float32(0.0))
        for t in range(n // tile)
    ]
    index = lax.broadcasted_iota(jnp.int32, (tile, 1), 0)
    for k in range(n):
        first = k // tile
        pivot_upper = upper[first][k % tile:k % tile + 1, :]
        pivot_lower = lower[first][k % tile:k % tile + 1, :]
        reciprocal = 1.0 / pivot_upper[:, k:k + 1]
        for t in range(first, n // tile):
            scale = upper[t][:, k:k + 1] * reciprocal
            if t == first:
                scale = jnp.where(index + t * tile > k, scale, jnp.float32(0.0))
            upper[t] = upper[t] - scale * pivot_upper
            lower[t] = lower[t] - scale * pivot_lower
    upper = jnp.concatenate(upper, axis=0)
    lower = jnp.concatenate(lower, axis=0)
    rows = lax.broadcasted_iota(jnp.int32, (n, n), 0)
    cols = lax.broadcasted_iota(jnp.int32, (n, n), 1)
    diagonal = jnp.sum(jnp.where(rows == cols, upper, 0.0), axis=1, keepdims=True)
    root = jnp.sqrt(diagonal)
    factor_ref[...] = jnp.where(rows <= cols, upper, 0.0) / root
    inverse_ref[...] = lower / root


def factor_and_invert(block):
    n = block.shape[0]
    return pl.pallas_call(
        _factor_kernel,
        out_shape=(
            jax.ShapeDtypeStruct((n, n), jnp.float32),
            jax.ShapeDtypeStruct((n, n), jnp.float32),
        ),
    )(block)


def on_device(normal_matrix, right_sides):
    row_blocks, _, block, col_blocks, _, _ = normal_matrix.shape
    col_id = lax.axis_index("col")
    row_id = lax.axis_index("row")
    col_count = lax.axis_size("col")
    row_count = lax.axis_size("row")
    side_count = right_sides.shape[0]
    local = normal_matrix.reshape(row_blocks * block, col_blocks * block)

    def factor(corner_raw):
        corner_t, inverse = factor_and_invert(corner_raw)
        return corner_t.T, inverse

    def skip(corner_raw):
        return jnp.zeros_like(corner_raw), jnp.zeros_like(corner_raw)

    holder = (row_id == 0) & (col_id == 0)
    corner, inverse = lax.cond(holder, factor, skip, local[:block, :block])
    left = spread(local[:, :block], "col")
    top = jnp.concatenate([local[:block], right_sides[:, 0, 0, :].T], axis=1)
    top = spread_wide(top, "row")
    inverse = spread_wide(inverse, "row")
    inverse, top = lax.optimization_barrier((inverse, top))
    inverse = spread_wide(inverse, "col")

    rows_factor = jnp.dot(
        left, inverse.T, precision=lax.Precision.HIGHEST, preferred_element_type=jnp.float32
    )
    solved = jnp.dot(
        inverse, top, precision=lax.Precision.HIGHEST, preferred_element_type=jnp.float32
    ).T
    cols_factor = solved[: col_blocks * block]
    lead = solved[col_blocks * block:]

    change = jnp.dot(
        rows_factor,
        cols_factor.T,
        precision=lax.Precision.HIGHEST,
        preferred_element_type=jnp.float32,
    )
    trailing = (local - change).reshape(row_blocks, block, col_blocks, block)
    global_rows = row_id + row_count * jnp.arange(row_blocks, dtype=jnp.int32)
    global_cols = col_id + col_count * jnp.arange(col_blocks, dtype=jnp.int32)
    inner = (global_rows[:, None, None, None] >= 1) & (global_cols[None, None, :, None] >= 1)
    result = jnp.where(inner, trailing, jnp.float32(0.0))
    column = jnp.where(
        global_rows[:, None, None] == 0, corner[None], rows_factor.reshape(row_blocks, block, block)
    )
    result = jnp.where((global_cols == 0)[None, None, :, None], column[:, :, None, :], result)
    result = result.reshape(normal_matrix.shape)

    flat = right_sides.reshape(side_count, row_blocks * block)
    reduced = flat - jnp.dot(
        lead, rows_factor.T, precision=lax.Precision.HIGHEST, preferred_element_type=jnp.float32
    )
    reduced = reduced.reshape(side_count, row_blocks, block)
    reduced = jnp.where((global_rows == 0)[None, :, None], lead[:, None, :], reduced)
    return (result, reduced.reshape(right_sides.shape))


def solution(mesh):
    placed = (P(None, "row", None, None, "col", None), P("col", None, "row", None))
    return jax.shard_map(
        on_device,
        mesh=mesh,
        in_specs=placed,
        out_specs=(P(None, "row", None, None, "col", None), P("col", None, "row", None)),
        check_vma=False,
    )
```

```python
import jax
import jax.numpy as jnp
from jax import lax
from jax.experimental import pallas as pl
from jax.sharding import PartitionSpec as P


def spread(block, axis):
    count = lax.axis_size(axis)
    index = lax.axis_index(axis)
    step = 1
    while 2 * step < count:
        step *= 2
    while step >= 1:
        pairs = [(i, i + step) for i in range(0, count, 2 * step) if i + step < count]
        arrived = lax.ppermute(block, axis, pairs)
        block = jnp.where(index % (2 * step) == step, arrived, block)
        step //= 2
    return block


def spread_wide(block, axis):
    count = lax.axis_size(axis)
    index = lax.axis_index(axis)
    radices = []
    rest = count
    while rest > 1:
        radix = 4 if rest % 4 == 0 else rest
        radices.append(radix)
        rest //= radix
    span = count
    for radix in radices:
        span //= radix
        got = block
        for digit in range(1, radix):
            pairs = [(i, i + digit * span) for i in range(0, count, span * radix)]
            arrived = lax.ppermute(block, axis, pairs)
            mine = (index % (span * radix)) == digit * span
            got = jnp.where(mine, arrived, got)
        block = got
    return block


def _factor_kernel(block_ref, factor_ref, inverse_ref):
    n = block_ref.shape[0]
    rows = lax.broadcasted_iota(jnp.int32, (n, n), 0)
    cols = lax.broadcasted_iota(jnp.int32, (n, n), 1)
    upper = block_ref[...]
    lower = jnp.where(rows == cols, jnp.float32(1.0), jnp.float32(0.0))
    index = lax.broadcasted_iota(jnp.int32, (n, 1), 0)
    for k in range(n):
        pivot_upper = upper[k:k + 1, :]
        pivot_lower = lower[k:k + 1, :]
        scale = jnp.where(
            index > k, upper[:, k:k + 1] / pivot_upper[:, k:k + 1], jnp.float32(0.0)
        )
        upper = upper - scale * pivot_upper
        lower = lower - scale * pivot_lower
    diagonal = jnp.sum(jnp.where(rows == cols, upper, 0.0), axis=1, keepdims=True)
    root = jnp.sqrt(diagonal)
    factor_ref[...] = jnp.where(rows <= cols, upper, 0.0) / root
    inverse_ref[...] = lower / root


def factor_and_invert(block):
    n = block.shape[0]
    return pl.pallas_call(
        _factor_kernel,
        out_shape=(
            jax.ShapeDtypeStruct((n, n), jnp.float32),
            jax.ShapeDtypeStruct((n, n), jnp.float32),
        ),
    )(block)


def on_device(normal_matrix, right_sides):
    row_blocks, _, block, col_blocks, _, _ = normal_matrix.shape
    col_id = lax.axis_index("col")
    row_id = lax.axis_index("row")
    col_count = lax.axis_size("col")
    row_count = lax.axis_size("row")
    side_count = right_sides.shape[0]
    local = normal_matrix.reshape(row_blocks * block, col_blocks * block)

    def factor(corner_raw):
        corner_t, inverse = factor_and_invert(corner_raw)
        return corner_t.T, inverse

    def skip(corner_raw):
        return jnp.zeros_like(corner_raw), jnp.zeros_like(corner_raw)

    holder = (row_id == 0) & (col_id == 0)
    corner, inverse = lax.cond(holder, factor, skip, local[:block, :block])
    inverse = spread_wide(spread_wide(inverse, "row"), "col")
    left = spread(local[:, :block], "col")
    top = jnp.concatenate([local[:block], right_sides[:, 0, 0, :].T], axis=1)
    top = spread(top, "row")

    rows_factor = jnp.dot(
        left, inverse.T, precision=lax.Precision.HIGHEST, preferred_element_type=jnp.float32
    )
    solved = jnp.dot(
        inverse, top, precision=lax.Precision.HIGHEST, preferred_element_type=jnp.float32
    ).T
    cols_factor = solved[: col_blocks * block]
    lead = solved[col_blocks * block:]

    change = jnp.dot(
        rows_factor,
        cols_factor.T,
        precision=lax.Precision.HIGHEST,
        preferred_element_type=jnp.float32,
    )
    trailing = (local - change).reshape(row_blocks, block, col_blocks, block)
    global_rows = row_id + row_count * jnp.arange(row_blocks, dtype=jnp.int32)
    global_cols = col_id + col_count * jnp.arange(col_blocks, dtype=jnp.int32)
    inner = (global_rows[:, None, None, None] >= 1) & (global_cols[None, None, :, None] >= 1)
    result = jnp.where(inner, trailing, jnp.float32(0.0))
    column = jnp.where(
        global_rows[:, None, None] == 0, corner[None], rows_factor.reshape(row_blocks, block, block)
    )
    result = jnp.where((global_cols == 0)[None, None, :, None], column[:, :, None, :], result)
    result = result.reshape(normal_matrix.shape)

    flat = right_sides.reshape(side_count, row_blocks * block)
    reduced = flat - jnp.dot(
        lead, rows_factor.T, precision=lax.Precision.HIGHEST, preferred_element_type=jnp.float32
    )
    reduced = reduced.reshape(side_count, row_blocks, block)
    reduced = jnp.where((global_rows == 0)[None, :, None], lead[:, None, :], reduced)
    return (result, reduced.reshape(right_sides.shape))


def solution(mesh):
    placed = (P(None, "row", None, None, "col", None), P("col", None, "row", None))
    return jax.shard_map(
        on_device,
        mesh=mesh,
        in_specs=placed,
        out_specs=(P(None, "row", None, None, "col", None), P("col", None, "row", None)),
        check_vma=False,
    )
```

```python
import jax
import jax.numpy as jnp
from jax import lax
from jax.experimental import pallas as pl
from jax.sharding import PartitionSpec as P


def spread(block, axis):
    count = lax.axis_size(axis)
    index = lax.axis_index(axis)
    step = 1
    while 2 * step < count:
        step *= 2
    while step >= 1:
        pairs = [(i, i + step) for i in range(0, count, 2 * step) if i + step < count]
        arrived = lax.ppermute(block, axis, pairs)
        block = jnp.where(index % (2 * step) == step, arrived, block)
        step //= 2
    return block


def spread_wide(block, axis):
    count = lax.axis_size(axis)
    index = lax.axis_index(axis)
    radices = []
    rest = count
    while rest > 1:
        radix = 4 if rest % 4 == 0 else rest
        radices.append(radix)
        rest //= radix
    span = count
    for radix in radices:
        span //= radix
        got = block
        for digit in range(1, radix):
            pairs = [(i, i + digit * span) for i in range(0, count, span * radix)]
            arrived = lax.ppermute(block, axis, pairs)
            mine = (index % (span * radix)) == digit * span
            got = jnp.where(mine, arrived, got)
        block = got
    return block


def _factor_kernel(block_ref, factor_ref, inverse_ref):
    n = block_ref.shape[0]
    rows = lax.broadcasted_iota(jnp.int32, (n, n), 0)
    cols = lax.broadcasted_iota(jnp.int32, (n, n), 1)
    upper = block_ref[...]
    lower = jnp.where(rows == cols, jnp.float32(1.0), jnp.float32(0.0))
    index = lax.broadcasted_iota(jnp.int32, (n, 1), 0)
    for k in range(n):
        pivot_upper = upper[k:k + 1, :]
        pivot_lower = lower[k:k + 1, :]
        scale = jnp.where(
            index > k, upper[:, k:k + 1] / pivot_upper[:, k:k + 1], jnp.float32(0.0)
        )
        upper = upper - scale * pivot_upper
        lower = lower - scale * pivot_lower
    diagonal = jnp.sum(jnp.where(rows == cols, upper, 0.0), axis=1, keepdims=True)
    root = jnp.sqrt(diagonal)
    factor_ref[...] = jnp.where(rows <= cols, upper, 0.0) / root
    inverse_ref[...] = lower / root


def factor_and_invert(block):
    n = block.shape[0]
    return pl.pallas_call(
        _factor_kernel,
        out_shape=(
            jax.ShapeDtypeStruct((n, n), jnp.float32),
            jax.ShapeDtypeStruct((n, n), jnp.float32),
        ),
    )(block)


def on_device(normal_matrix, right_sides):
    row_blocks, _, block, col_blocks, _, _ = normal_matrix.shape
    col_id = lax.axis_index("col")
    row_id = lax.axis_index("row")
    col_count = lax.axis_size("col")
    row_count = lax.axis_size("row")
    side_count = right_sides.shape[0]
    local = normal_matrix.reshape(row_blocks * block, col_blocks * block)

    def factor(corner_raw):
        corner_t, inverse = factor_and_invert(corner_raw)
        return corner_t.T, inverse

    def skip(corner_raw):
        return jnp.zeros_like(corner_raw), jnp.zeros_like(corner_raw)

    holder = (row_id == 0) & (col_id == 0)
    corner, inverse = lax.cond(holder, factor, skip, local[:block, :block])
    inverse = spread(spread(inverse, "row"), "col")
    left = spread(local[:, :block], "col")
    top = jnp.concatenate([local[:block], right_sides[:, 0, 0, :].T], axis=1)
    top = spread(top, "row")

    rows_factor = jnp.dot(
        left, inverse.T, precision=lax.Precision.HIGHEST, preferred_element_type=jnp.float32
    )
    solved = jnp.dot(
        inverse, top, precision=lax.Precision.HIGHEST, preferred_element_type=jnp.float32
    ).T
    cols_factor = solved[: col_blocks * block]
    lead = solved[col_blocks * block:]

    change = jnp.dot(
        rows_factor,
        cols_factor.T,
        precision=lax.Precision.HIGHEST,
        preferred_element_type=jnp.float32,
    )
    trailing = (local - change).reshape(row_blocks, block, col_blocks, block)
    global_rows = row_id + row_count * jnp.arange(row_blocks, dtype=jnp.int32)
    global_cols = col_id + col_count * jnp.arange(col_blocks, dtype=jnp.int32)
    inner = (global_rows[:, None, None, None] >= 1) & (global_cols[None, None, :, None] >= 1)
    result = jnp.where(inner, trailing, jnp.float32(0.0))
    column = jnp.where(
        global_rows[:, None, None] == 0, corner[None], rows_factor.reshape(row_blocks, block, block)
    )
    result = jnp.where((global_cols == 0)[None, None, :, None], column[:, :, None, :], result)
    result = result.reshape(normal_matrix.shape)

    flat = right_sides.reshape(side_count, row_blocks * block)
    reduced = flat - jnp.dot(
        lead, rows_factor.T, precision=lax.Precision.HIGHEST, preferred_element_type=jnp.float32
    )
    reduced = reduced.reshape(side_count, row_blocks, block)
    reduced = jnp.where((global_rows == 0)[None, :, None], lead[:, None, :], reduced)
    return (result, reduced.reshape(right_sides.shape))


def solution(mesh):
    placed = (P(None, "row", None, None, "col", None), P("col", None, "row", None))
    return jax.shard_map(
        on_device,
        mesh=mesh,
        in_specs=placed,
        out_specs=(P(None, "row", None, None, "col", None), P("col", None, "row", None)),
        check_vma=False,
    )
```

```python
import jax
import jax.numpy as jnp
from jax import lax
from jax.experimental import pallas as pl
from jax.sharding import PartitionSpec as P


def spread(block, axis):
    count = lax.axis_size(axis)
    index = lax.axis_index(axis)
    step = 1
    while 2 * step < count:
        step *= 2
    while step >= 1:
        pairs = [(i, i + step) for i in range(0, count, 2 * step) if i + step < count]
        arrived = lax.ppermute(block, axis, pairs)
        block = jnp.where(index % (2 * step) == step, arrived, block)
        step //= 2
    return block


def spread_wide(block, axis):
    count = lax.axis_size(axis)
    index = lax.axis_index(axis)
    radices = []
    rest = count
    while rest > 1:
        radix = 4 if rest % 4 == 0 else rest
        radices.append(radix)
        rest //= radix
    span = count
    for radix in radices:
        span //= radix
        got = block
        for digit in range(1, radix):
            pairs = [(i, i + digit * span) for i in range(0, count, span * radix)]
            arrived = lax.ppermute(block, axis, pairs)
            mine = (index % (span * radix)) == digit * span
            got = jnp.where(mine, arrived, got)
        block = got
    return block


def _factor_kernel(block_ref, factor_ref, inverse_ref):
    n = block_ref.shape[0]
    rows = lax.broadcasted_iota(jnp.int32, (n, n), 0)
    cols = lax.broadcasted_iota(jnp.int32, (n, n), 1)
    upper = block_ref[...]
    lower = jnp.where(rows == cols, jnp.float32(1.0), jnp.float32(0.0))
    index = lax.broadcasted_iota(jnp.int32, (n, 1), 0)
    for k in range(n):
        pivot_upper = upper[k:k + 1, :]
        pivot_lower = lower[k:k + 1, :]
        scale = jnp.where(
            index > k, upper[:, k:k + 1] / pivot_upper[:, k:k + 1], jnp.float32(0.0)
        )
        upper = upper - scale * pivot_upper
        lower = lower - scale * pivot_lower
    diagonal = jnp.sum(jnp.where(rows == cols, upper, 0.0), axis=1, keepdims=True)
    root = jnp.sqrt(diagonal)
    factor_ref[...] = jnp.where(rows <= cols, upper, 0.0) / root
    inverse_ref[...] = lower / root


def factor_and_invert(block):
    n = block.shape[0]
    return pl.pallas_call(
        _factor_kernel,
        out_shape=(
            jax.ShapeDtypeStruct((n, n), jnp.float32),
            jax.ShapeDtypeStruct((n, n), jnp.float32),
        ),
    )(block)


def on_device(normal_matrix, right_sides):
    row_blocks, _, block, col_blocks, _, _ = normal_matrix.shape
    col_id = lax.axis_index("col")
    row_id = lax.axis_index("row")
    col_count = lax.axis_size("col")
    row_count = lax.axis_size("row")
    side_count = right_sides.shape[0]
    local = normal_matrix.reshape(row_blocks * block, col_blocks * block)

    def factor(corner_raw):
        corner_t, inverse = factor_and_invert(corner_raw)
        return corner_t.T, inverse

    def skip(corner_raw):
        return jnp.zeros_like(corner_raw), jnp.zeros_like(corner_raw)

    holder = (row_id == 0) & (col_id == 0)
    corner, inverse = lax.cond(holder, factor, skip, local[:block, :block])
    inverse = spread(spread_wide(inverse, "row"), "col")
    left = spread(local[:, :block], "col")
    top = jnp.concatenate([local[:block], right_sides[:, 0, 0, :].T], axis=1)
    top = spread(top, "row")

    rows_factor = jnp.dot(
        left, inverse.T, precision=lax.Precision.HIGHEST, preferred_element_type=jnp.float32
    )
    solved = jnp.dot(
        inverse, top, precision=lax.Precision.HIGHEST, preferred_element_type=jnp.float32
    ).T
    cols_factor = solved[: col_blocks * block]
    lead = solved[col_blocks * block:]

    change = jnp.dot(
        rows_factor,
        cols_factor.T,
        precision=lax.Precision.HIGHEST,
        preferred_element_type=jnp.float32,
    )
    trailing = (local - change).reshape(row_blocks, block, col_blocks, block)
    global_rows = row_id + row_count * jnp.arange(row_blocks, dtype=jnp.int32)
    global_cols = col_id + col_count * jnp.arange(col_blocks, dtype=jnp.int32)
    inner = (global_rows[:, None, None, None] >= 1) & (global_cols[None, None, :, None] >= 1)
    result = jnp.where(inner, trailing, jnp.float32(0.0))
    column = jnp.where(
        global_rows[:, None, None] == 0, corner[None], rows_factor.reshape(row_blocks, block, block)
    )
    result = jnp.where((global_cols == 0)[None, None, :, None], column[:, :, None, :], result)
    result = result.reshape(normal_matrix.shape)

    flat = right_sides.reshape(side_count, row_blocks * block)
    reduced = flat - jnp.dot(
        lead, rows_factor.T, precision=lax.Precision.HIGHEST, preferred_element_type=jnp.float32
    )
    reduced = reduced.reshape(side_count, row_blocks, block)
    reduced = jnp.where((global_rows == 0)[None, :, None], lead[:, None, :], reduced)
    return (result, reduced.reshape(right_sides.shape))


def solution(mesh):
    placed = (P(None, "row", None, None, "col", None), P("col", None, "row", None))
    return jax.shard_map(
        on_device,
        mesh=mesh,
        in_specs=placed,
        out_specs=(P(None, "row", None, None, "col", None), P("col", None, "row", None)),
        check_vma=False,
    )
```

```python
import jax
import jax.numpy as jnp
from jax import lax
from jax.experimental import pallas as pl
from jax.sharding import PartitionSpec as P


def spread(block, axis):
    count = lax.axis_size(axis)
    index = lax.axis_index(axis)
    step = 1
    while 2 * step < count:
        step *= 2
    while step >= 1:
        pairs = [(i, i + step) for i in range(0, count, 2 * step) if i + step < count]
        arrived = lax.ppermute(block, axis, pairs)
        block = jnp.where(index % (2 * step) == step, arrived, block)
        step //= 2
    return block


def spread_wide(block, axis):
    count = lax.axis_size(axis)
    index = lax.axis_index(axis)
    radices = []
    rest = count
    while rest > 1:
        radix = 4 if rest % 4 == 0 else rest
        radices.append(radix)
        rest //= radix
    span = count
    for radix in radices:
        span //= radix
        got = block
        for digit in range(1, radix):
            pairs = [(i, i + digit * span) for i in range(0, count, span * radix)]
            arrived = lax.ppermute(block, axis, pairs)
            mine = (index % (span * radix)) == digit * span
            got = jnp.where(mine, arrived, got)
        block = got
    return block


def _factor_kernel(block_ref, factor_ref, inverse_ref):
    n = block_ref.shape[0]
    rows = lax.broadcasted_iota(jnp.int32, (n, n), 0)
    cols = lax.broadcasted_iota(jnp.int32, (n, n), 1)
    upper = block_ref[...]
    lower = jnp.where(rows == cols, jnp.float32(1.0), jnp.float32(0.0))
    index = lax.broadcasted_iota(jnp.int32, (n, 1), 0)
    for k in range(n):
        pivot_upper = upper[k:k + 1, :]
        pivot_lower = lower[k:k + 1, :]
        scale = jnp.where(
            index > k, upper[:, k:k + 1] / pivot_upper[:, k:k + 1], jnp.float32(0.0)
        )
        upper = upper - scale * pivot_upper
        lower = lower - scale * pivot_lower
    diagonal = jnp.sum(jnp.where(rows == cols, upper, 0.0), axis=1, keepdims=True)
    root = jnp.sqrt(diagonal)
    factor_ref[...] = jnp.where(rows <= cols, upper, 0.0) / root
    inverse_ref[...] = lower / root


def factor_and_invert(block):
    n = block.shape[0]
    return pl.pallas_call(
        _factor_kernel,
        out_shape=(
            jax.ShapeDtypeStruct((n, n), jnp.float32),
            jax.ShapeDtypeStruct((n, n), jnp.float32),
        ),
    )(block)


def on_device(normal_matrix, right_sides):
    row_blocks, _, block, col_blocks, _, _ = normal_matrix.shape
    col_id = lax.axis_index("col")
    row_id = lax.axis_index("row")
    col_count = lax.axis_size("col")
    row_count = lax.axis_size("row")
    side_count = right_sides.shape[0]
    local = normal_matrix.reshape(row_blocks * block, col_blocks * block)

    def factor(corner_raw):
        corner_t, inverse = factor_and_invert(corner_raw)
        return corner_t.T, inverse

    def skip(corner_raw):
        return jnp.zeros_like(corner_raw), jnp.zeros_like(corner_raw)

    holder = (row_id == 0) & (col_id == 0)
    corner, inverse = lax.cond(holder, factor, skip, local[:block, :block])
    inverse = spread_wide(spread_wide(inverse, "col"), "row")
    left = spread(local[:, :block], "col")
    top = jnp.concatenate([local[:block], right_sides[:, 0, 0, :].T], axis=1)
    top = spread(top, "row")

    rows_factor = jnp.dot(
        left, inverse.T, precision=lax.Precision.HIGHEST, preferred_element_type=jnp.float32
    )
    solved = jnp.dot(
        inverse, top, precision=lax.Precision.HIGHEST, preferred_element_type=jnp.float32
    ).T
    cols_factor = solved[: col_blocks * block]
    lead = solved[col_blocks * block:]

    change = jnp.dot(
        rows_factor,
        cols_factor.T,
        precision=lax.Precision.HIGHEST,
        preferred_element_type=jnp.float32,
    )
    trailing = (local - change).reshape(row_blocks, block, col_blocks, block)
    global_rows = row_id + row_count * jnp.arange(row_blocks, dtype=jnp.int32)
    global_cols = col_id + col_count * jnp.arange(col_blocks, dtype=jnp.int32)
    inner = (global_rows[:, None, None, None] >= 1) & (global_cols[None, None, :, None] >= 1)
    result = jnp.where(inner, trailing, jnp.float32(0.0))
    column = jnp.where(
        global_rows[:, None, None] == 0, corner[None], rows_factor.reshape(row_blocks, block, block)
    )
    result = jnp.where((global_cols == 0)[None, None, :, None], column[:, :, None, :], result)
    result = result.reshape(normal_matrix.shape)

    flat = right_sides.reshape(side_count, row_blocks * block)
    reduced = flat - jnp.dot(
        lead, rows_factor.T, precision=lax.Precision.HIGHEST, preferred_element_type=jnp.float32
    )
    reduced = reduced.reshape(side_count, row_blocks, block)
    reduced = jnp.where((global_rows == 0)[None, :, None], lead[:, None, :], reduced)
    return (result, reduced.reshape(right_sides.shape))


def solution(mesh):
    placed = (P(None, "row", None, None, "col", None), P("col", None, "row", None))
    return jax.shard_map(
        on_device,
        mesh=mesh,
        in_specs=placed,
        out_specs=(P(None, "row", None, None, "col", None), P("col", None, "row", None)),
        check_vma=False,
    )
```

```python
import jax
import jax.numpy as jnp
from jax import lax
from jax.experimental import pallas as pl
from jax.sharding import PartitionSpec as P


def spread(block, axis):
    count = lax.axis_size(axis)
    index = lax.axis_index(axis)
    step = 1
    while 2 * step < count:
        step *= 2
    while step >= 1:
        pairs = [(i, i + step) for i in range(0, count, 2 * step) if i + step < count]
        arrived = lax.ppermute(block, axis, pairs)
        block = jnp.where(index % (2 * step) == step, arrived, block)
        step //= 2
    return block


def spread_wide(block, axis):
    count = lax.axis_size(axis)
    index = lax.axis_index(axis)
    radices = []
    rest = count
    while rest > 1:
        radix = 4 if rest % 4 == 0 else rest
        radices.append(radix)
        rest //= radix
    span = count
    for radix in radices:
        span //= radix
        got = block
        for digit in range(1, radix):
            pairs = [(i, i + digit * span) for i in range(0, count, span * radix)]
            arrived = lax.ppermute(block, axis, pairs)
            mine = (index % (span * radix)) == digit * span
            got = jnp.where(mine, arrived, got)
        block = got
    return block


def _factor_kernel(block_ref, factor_ref, inverse_ref):
    n = block_ref.shape[0]
    rows = lax.broadcasted_iota(jnp.int32, (n, n), 0)
    cols = lax.broadcasted_iota(jnp.int32, (n, n), 1)
    upper = block_ref[...]
    lower = jnp.where(rows == cols, jnp.float32(1.0), jnp.float32(0.0))
    index = lax.broadcasted_iota(jnp.int32, (n, 1), 0)
    for k in range(n):
        pivot_upper = upper[k:k + 1, :]
        pivot_lower = lower[k:k + 1, :]
        scale = jnp.where(
            index > k, upper[:, k:k + 1] / pivot_upper[:, k:k + 1], jnp.float32(0.0)
        )
        upper = upper - scale * pivot_upper
        lower = lower - scale * pivot_lower
    diagonal = jnp.sum(jnp.where(rows == cols, upper, 0.0), axis=1, keepdims=True)
    root = jnp.sqrt(diagonal)
    factor_ref[...] = jnp.where(rows <= cols, upper, 0.0) / root
    inverse_ref[...] = lower / root


def factor_and_invert(block):
    n = block.shape[0]
    return pl.pallas_call(
        _factor_kernel,
        out_shape=(
            jax.ShapeDtypeStruct((n, n), jnp.float32),
            jax.ShapeDtypeStruct((n, n), jnp.float32),
        ),
    )(block)


def on_device(normal_matrix, right_sides):
    row_blocks, _, block, col_blocks, _, _ = normal_matrix.shape
    col_id = lax.axis_index("col")
    row_id = lax.axis_index("row")
    col_count = lax.axis_size("col")
    row_count = lax.axis_size("row")
    side_count = right_sides.shape[0]
    local = normal_matrix.reshape(row_blocks * block, col_blocks * block)

    def factor(corner_raw):
        corner_t, inverse = factor_and_invert(corner_raw)
        return corner_t.T, inverse

    def skip(corner_raw):
        return jnp.zeros_like(corner_raw), jnp.zeros_like(corner_raw)

    holder = (row_id == 0) & (col_id == 0)
    corner, inverse = lax.cond(holder, factor, skip, local[:block, :block])
    inverse = spread_wide(spread_wide(inverse, "col"), "row")
    left = spread_wide(local[:, :block], "col")
    top = jnp.concatenate([local[:block], right_sides[:, 0, 0, :].T], axis=1)
    top = spread(top, "row")

    rows_factor = jnp.dot(
        left, inverse.T, precision=lax.Precision.HIGHEST, preferred_element_type=jnp.float32
    )
    solved = jnp.dot(
        inverse, top, precision=lax.Precision.HIGHEST, preferred_element_type=jnp.float32
    ).T
    cols_factor = solved[: col_blocks * block]
    lead = solved[col_blocks * block:]

    change = jnp.dot(
        rows_factor,
        cols_factor.T,
        precision=lax.Precision.HIGHEST,
        preferred_element_type=jnp.float32,
    )
    trailing = (local - change).reshape(row_blocks, block, col_blocks, block)
    global_rows = row_id + row_count * jnp.arange(row_blocks, dtype=jnp.int32)
    global_cols = col_id + col_count * jnp.arange(col_blocks, dtype=jnp.int32)
    inner = (global_rows[:, None, None, None] >= 1) & (global_cols[None, None, :, None] >= 1)
    result = jnp.where(inner, trailing, jnp.float32(0.0))
    column = jnp.where(
        global_rows[:, None, None] == 0, corner[None], rows_factor.reshape(row_blocks, block, block)
    )
    result = jnp.where((global_cols == 0)[None, None, :, None], column[:, :, None, :], result)
    result = result.reshape(normal_matrix.shape)

    flat = right_sides.reshape(side_count, row_blocks * block)
    reduced = flat - jnp.dot(
        lead, rows_factor.T, precision=lax.Precision.HIGHEST, preferred_element_type=jnp.float32
    )
    reduced = reduced.reshape(side_count, row_blocks, block)
    reduced = jnp.where((global_rows == 0)[None, :, None], lead[:, None, :], reduced)
    return (result, reduced.reshape(right_sides.shape))


def solution(mesh):
    placed = (P(None, "row", None, None, "col", None), P("col", None, "row", None))
    return jax.shard_map(
        on_device,
        mesh=mesh,
        in_specs=placed,
        out_specs=(P(None, "row", None, None, "col", None), P("col", None, "row", None)),
        check_vma=False,
    )
```

```python
import jax
import jax.numpy as jnp
from jax import lax
from jax.experimental import pallas as pl
from jax.sharding import PartitionSpec as P


def spread(block, axis):
    count = lax.axis_size(axis)
    index = lax.axis_index(axis)
    step = 1
    while 2 * step < count:
        step *= 2
    while step >= 1:
        pairs = [(i, i + step) for i in range(0, count, 2 * step) if i + step < count]
        arrived = lax.ppermute(block, axis, pairs)
        block = jnp.where(index % (2 * step) == step, arrived, block)
        step //= 2
    return block


def spread_wide(block, axis):
    count = lax.axis_size(axis)
    index = lax.axis_index(axis)
    radices = []
    rest = count
    while rest > 1:
        radix = 4 if rest % 4 == 0 else rest
        radices.append(radix)
        rest //= radix
    span = count
    for radix in radices:
        span //= radix
        got = block
        for digit in range(radix - 1, 0, -1):
            pairs = [(i, i + digit * span) for i in range(0, count, span * radix)]
            arrived = lax.ppermute(block, axis, pairs)
            mine = (index % (span * radix)) == digit * span
            got = jnp.where(mine, arrived, got)
        block = got
    return block


def _factor_kernel(block_ref, factor_ref, inverse_ref):
    n = block_ref.shape[0]
    rows = lax.broadcasted_iota(jnp.int32, (n, n), 0)
    cols = lax.broadcasted_iota(jnp.int32, (n, n), 1)
    upper = block_ref[...]
    lower = jnp.where(rows == cols, jnp.float32(1.0), jnp.float32(0.0))
    index = lax.broadcasted_iota(jnp.int32, (n, 1), 0)
    for k in range(n):
        pivot_upper = upper[k:k + 1, :]
        pivot_lower = lower[k:k + 1, :]
        scale = jnp.where(
            index > k, upper[:, k:k + 1] / pivot_upper[:, k:k + 1], jnp.float32(0.0)
        )
        upper = upper - scale * pivot_upper
        lower = lower - scale * pivot_lower
    diagonal = jnp.sum(jnp.where(rows == cols, upper, 0.0), axis=1, keepdims=True)
    root = jnp.sqrt(diagonal)
    factor_ref[...] = jnp.where(rows <= cols, upper, 0.0) / root
    inverse_ref[...] = lower / root


def factor_and_invert(block):
    n = block.shape[0]
    return pl.pallas_call(
        _factor_kernel,
        out_shape=(
            jax.ShapeDtypeStruct((n, n), jnp.float32),
            jax.ShapeDtypeStruct((n, n), jnp.float32),
        ),
    )(block)


def on_device(normal_matrix, right_sides):
    row_blocks, _, block, col_blocks, _, _ = normal_matrix.shape
    col_id = lax.axis_index("col")
    row_id = lax.axis_index("row")
    col_count = lax.axis_size("col")
    row_count = lax.axis_size("row")
    side_count = right_sides.shape[0]
    local = normal_matrix.reshape(row_blocks * block, col_blocks * block)

    def factor(corner_raw):
        corner_t, inverse = factor_and_invert(corner_raw)
        return corner_t.T, inverse

    def skip(corner_raw):
        return jnp.zeros_like(corner_raw), jnp.zeros_like(corner_raw)

    holder = (row_id == 0) & (col_id == 0)
    corner, inverse = lax.cond(holder, factor, skip, local[:block, :block])
    inverse = spread_wide(spread_wide(inverse, "col"), "row")
    left = spread(local[:, :block], "col")
    top = jnp.concatenate([local[:block], right_sides[:, 0, 0, :].T], axis=1)
    top = spread(top, "row")

    rows_factor = jnp.dot(
        left, inverse.T, precision=lax.Precision.HIGHEST, preferred_element_type=jnp.float32
    )
    solved = jnp.dot(
        inverse, top, precision=lax.Precision.HIGHEST, preferred_element_type=jnp.float32
    ).T
    cols_factor = solved[: col_blocks * block]
    lead = solved[col_blocks * block:]

    change = jnp.dot(
        rows_factor,
        cols_factor.T,
        precision=lax.Precision.HIGHEST,
        preferred_element_type=jnp.float32,
    )
    trailing = (local - change).reshape(row_blocks, block, col_blocks, block)
    global_rows = row_id + row_count * jnp.arange(row_blocks, dtype=jnp.int32)
    global_cols = col_id + col_count * jnp.arange(col_blocks, dtype=jnp.int32)
    inner = (global_rows[:, None, None, None] >= 1) & (global_cols[None, None, :, None] >= 1)
    result = jnp.where(inner, trailing, jnp.float32(0.0))
    column = jnp.where(
        global_rows[:, None, None] == 0, corner[None], rows_factor.reshape(row_blocks, block, block)
    )
    result = jnp.where((global_cols == 0)[None, None, :, None], column[:, :, None, :], result)
    result = result.reshape(normal_matrix.shape)

    flat = right_sides.reshape(side_count, row_blocks * block)
    reduced = flat - jnp.dot(
        lead, rows_factor.T, precision=lax.Precision.HIGHEST, preferred_element_type=jnp.float32
    )
    reduced = reduced.reshape(side_count, row_blocks, block)
    reduced = jnp.where((global_rows == 0)[None, :, None], lead[:, None, :], reduced)
    return (result, reduced.reshape(right_sides.shape))


def solution(mesh):
    placed = (P(None, "row", None, None, "col", None), P("col", None, "row", None))
    return jax.shard_map(
        on_device,
        mesh=mesh,
        in_specs=placed,
        out_specs=(P(None, "row", None, None, "col", None), P("col", None, "row", None)),
        check_vma=False,
    )
```

```python
import jax
import jax.numpy as jnp
from jax import lax
from jax.experimental import pallas as pl
from jax.sharding import PartitionSpec as P


def spread(block, axis):
    count = lax.axis_size(axis)
    index = lax.axis_index(axis)
    step = 1
    while 2 * step < count:
        step *= 2
    while step >= 1:
        pairs = [(i, i + step) for i in range(0, count, 2 * step) if i + step < count]
        arrived = lax.ppermute(block, axis, pairs)
        block = jnp.where(index % (2 * step) == step, arrived, block)
        step //= 2
    return block


def spread_wide(block, axis):
    count = lax.axis_size(axis)
    index = lax.axis_index(axis)
    radices = []
    rest = count
    while rest > 1:
        radix = 4 if rest % 4 == 0 else rest
        radices.append(radix)
        rest //= radix
    span = count
    for radix in radices:
        span //= radix
        got = block
        for digit in range(1, radix):
            pairs = [(i, i + digit * span) for i in range(0, count, span * radix)]
            arrived = lax.ppermute(block, axis, pairs)
            mine = (index % (span * radix)) == digit * span
            got = jnp.where(mine, arrived, got)
        block = got
    return block


def _factor_kernel(block_ref, factor_ref, inverse_ref):
    n = block_ref.shape[0]
    rows = lax.broadcasted_iota(jnp.int32, (n, n), 0)
    cols = lax.broadcasted_iota(jnp.int32, (n, n), 1)
    upper = block_ref[...]
    lower = jnp.where(rows == cols, jnp.float32(1.0), jnp.float32(0.0))
    index = lax.broadcasted_iota(jnp.int32, (n, 1), 0)
    for k in range(n):
        pivot_upper = upper[k:k + 1, :]
        pivot_lower = lower[k:k + 1, :]
        scale = jnp.where(
            index > k, upper[:, k:k + 1] / pivot_upper[:, k:k + 1], jnp.float32(0.0)
        )
        upper = upper - scale * pivot_upper
        lower = lower - scale * pivot_lower
    diagonal = jnp.sum(jnp.where(rows == cols, upper, 0.0), axis=1, keepdims=True)
    root = jnp.sqrt(diagonal)
    factor_ref[...] = jnp.where(rows <= cols, upper, 0.0) / root
    inverse_ref[...] = lower / root


def factor_and_invert(block):
    n = block.shape[0]
    return pl.pallas_call(
        _factor_kernel,
        out_shape=(
            jax.ShapeDtypeStruct((n, n), jnp.float32),
            jax.ShapeDtypeStruct((n, n), jnp.float32),
        ),
    )(block)


def on_device(normal_matrix, right_sides):
    row_blocks, _, block, col_blocks, _, _ = normal_matrix.shape
    col_id = lax.axis_index("col")
    row_id = lax.axis_index("row")
    col_count = lax.axis_size("col")
    row_count = lax.axis_size("row")
    side_count = right_sides.shape[0]
    local = normal_matrix.reshape(row_blocks * block, col_blocks * block)

    def factor(corner_raw):
        corner_t, inverse = factor_and_invert(corner_raw)
        return corner_t.T, inverse

    def skip(corner_raw):
        return jnp.zeros_like(corner_raw), jnp.zeros_like(corner_raw)

    holder = (row_id == 0) & (col_id == 0)
    corner, inverse = lax.cond(holder, factor, skip, local[:block, :block])
    inverse = spread_wide(spread_wide(inverse, "col"), "row")
    left = spread(local[:, :block], "col")
    top = jnp.concatenate([local[:block], right_sides[:, 0, 0, :].T], axis=1)
    top = spread_wide(top, "row")

    rows_factor = jnp.dot(
        left, inverse.T, precision=lax.Precision.HIGHEST, preferred_element_type=jnp.float32
    )
    solved = jnp.dot(
        inverse, top, precision=lax.Precision.HIGHEST, preferred_element_type=jnp.float32
    ).T
    cols_factor = solved[: col_blocks * block]
    lead = solved[col_blocks * block:]

    change = jnp.dot(
        rows_factor,
        cols_factor.T,
        precision=lax.Precision.HIGHEST,
        preferred_element_type=jnp.float32,
    )
    trailing = (local - change).reshape(row_blocks, block, col_blocks, block)
    global_rows = row_id + row_count * jnp.arange(row_blocks, dtype=jnp.int32)
    global_cols = col_id + col_count * jnp.arange(col_blocks, dtype=jnp.int32)
    inner = (global_rows[:, None, None, None] >= 1) & (global_cols[None, None, :, None] >= 1)
    result = jnp.where(inner, trailing, jnp.float32(0.0))
    column = jnp.where(
        global_rows[:, None, None] == 0, corner[None], rows_factor.reshape(row_blocks, block, block)
    )
    result = jnp.where((global_cols == 0)[None, None, :, None], column[:, :, None, :], result)
    result = result.reshape(normal_matrix.shape)

    flat = right_sides.reshape(side_count, row_blocks * block)
    reduced = flat - jnp.dot(
        lead, rows_factor.T, precision=lax.Precision.HIGHEST, preferred_element_type=jnp.float32
    )
    reduced = reduced.reshape(side_count, row_blocks, block)
    reduced = jnp.where((global_rows == 0)[None, :, None], lead[:, None, :], reduced)
    return (result, reduced.reshape(right_sides.shape))


def solution(mesh):
    placed = (P(None, "row", None, None, "col", None), P("col", None, "row", None))
    return jax.shard_map(
        on_device,
        mesh=mesh,
        in_specs=placed,
        out_specs=(P(None, "row", None, None, "col", None), P("col", None, "row", None)),
        check_vma=False,
    )
```

```python
import jax
import jax.numpy as jnp
from jax import lax
from jax.experimental import pallas as pl
from jax.sharding import PartitionSpec as P


def spread(block, axis):
    count = lax.axis_size(axis)
    index = lax.axis_index(axis)
    step = 1
    while 2 * step < count:
        step *= 2
    while step >= 1:
        pairs = [(i, i + step) for i in range(0, count, 2 * step) if i + step < count]
        arrived = lax.ppermute(block, axis, pairs)
        block = jnp.where(index % (2 * step) == step, arrived, block)
        step //= 2
    return block


def spread_wide(block, axis):
    count = lax.axis_size(axis)
    index = lax.axis_index(axis)
    radices = []
    rest = count
    while rest > 1:
        radix = 4 if rest % 4 == 0 else rest
        radices.append(radix)
        rest //= radix
    span = count
    for radix in radices:
        span //= radix
        got = block
        for digit in range(1, radix):
            pairs = [(i, i + digit * span) for i in range(0, count, span * radix)]
            arrived = lax.ppermute(block, axis, pairs)
            mine = (index % (span * radix)) == digit * span
            got = jnp.where(mine, arrived, got)
        block = got
    return block


def _factor_kernel(block_ref, factor_ref, inverse_ref):
    n = block_ref.shape[0]
    rows = lax.broadcasted_iota(jnp.int32, (n, n), 0)
    cols = lax.broadcasted_iota(jnp.int32, (n, n), 1)
    upper = block_ref[...]
    lower = jnp.where(rows == cols, jnp.float32(1.0), jnp.float32(0.0))
    index = lax.broadcasted_iota(jnp.int32, (n, 1), 0)
    for k in range(n):
        pivot_upper = upper[k:k + 1, :]
        pivot_lower = lower[k:k + 1, :]
        scale = jnp.where(
            index > k, upper[:, k:k + 1] / pivot_upper[:, k:k + 1], jnp.float32(0.0)
        )
        upper = upper - scale * pivot_upper
        lower = lower - scale * pivot_lower
    diagonal = jnp.sum(jnp.where(rows == cols, upper, 0.0), axis=1, keepdims=True)
    root = jnp.sqrt(diagonal)
    factor_ref[...] = jnp.where(rows <= cols, upper, 0.0) / root
    inverse_ref[...] = lower / root


def factor_and_invert(block):
    n = block.shape[0]
    return pl.pallas_call(
        _factor_kernel,
        out_shape=(
            jax.ShapeDtypeStruct((n, n), jnp.float32),
            jax.ShapeDtypeStruct((n, n), jnp.float32),
        ),
    )(block)


def on_device(normal_matrix, right_sides):
    row_blocks, _, block, col_blocks, _, _ = normal_matrix.shape
    col_id = lax.axis_index("col")
    row_id = lax.axis_index("row")
    col_count = lax.axis_size("col")
    row_count = lax.axis_size("row")
    side_count = right_sides.shape[0]
    local = normal_matrix.reshape(row_blocks * block, col_blocks * block)

    def factor(corner_raw):
        corner_t, inverse = factor_and_invert(corner_raw)
        return corner_t.T, inverse

    def skip(corner_raw):
        return jnp.zeros_like(corner_raw), jnp.zeros_like(corner_raw)

    holder = (row_id == 0) & (col_id == 0)
    corner, inverse = lax.cond(holder, factor, skip, local[:block, :block])
    inverse = spread(spread_wide(inverse, "col"), "row")
    left = spread(local[:, :block], "col")
    top = jnp.concatenate([local[:block], right_sides[:, 0, 0, :].T], axis=1)
    top = spread(top, "row")

    rows_factor = jnp.dot(
        left, inverse.T, precision=lax.Precision.HIGHEST, preferred_element_type=jnp.float32
    )
    solved = jnp.dot(
        inverse, top, precision=lax.Precision.HIGHEST, preferred_element_type=jnp.float32
    ).T
    cols_factor = solved[: col_blocks * block]
    lead = solved[col_blocks * block:]

    change = jnp.dot(
        rows_factor,
        cols_factor.T,
        precision=lax.Precision.HIGHEST,
        preferred_element_type=jnp.float32,
    )
    trailing = (local - change).reshape(row_blocks, block, col_blocks, block)
    global_rows = row_id + row_count * jnp.arange(row_blocks, dtype=jnp.int32)
    global_cols = col_id + col_count * jnp.arange(col_blocks, dtype=jnp.int32)
    inner = (global_rows[:, None, None, None] >= 1) & (global_cols[None, None, :, None] >= 1)
    result = jnp.where(inner, trailing, jnp.float32(0.0))
    column = jnp.where(
        global_rows[:, None, None] == 0, corner[None], rows_factor.reshape(row_blocks, block, block)
    )
    result = jnp.where((global_cols == 0)[None, None, :, None], column[:, :, None, :], result)
    result = result.reshape(normal_matrix.shape)

    flat = right_sides.reshape(side_count, row_blocks * block)
    reduced = flat - jnp.dot(
        lead, rows_factor.T, precision=lax.Precision.HIGHEST, preferred_element_type=jnp.float32
    )
    reduced = reduced.reshape(side_count, row_blocks, block)
    reduced = jnp.where((global_rows == 0)[None, :, None], lead[:, None, :], reduced)
    return (result, reduced.reshape(right_sides.shape))


def solution(mesh):
    placed = (P(None, "row", None, None, "col", None), P("col", None, "row", None))
    return jax.shard_map(
        on_device,
        mesh=mesh,
        in_specs=placed,
        out_specs=(P(None, "row", None, None, "col", None), P("col", None, "row", None)),
        check_vma=False,
    )
```
